128 devices in a mesh: rows: 32 (over y, x, core), rep: 4 (over z).
Axes of the slice: x: 4, y: 4, z: 4, core: 2. Of those that a mesh axis runs over, the one named last changes fastest.
Arguments:
- weights: bfloat16 [80, 2097152], P('rep', 'rows'), may hold values from 0.25 to 4
- cell_ids: int32 [2097152], P('rows'), may hold values from 0 to 31
- group_sizes: int32 [32, 1024], P('rows'), may hold values from 32 to 96, as said below
- group_county: int32 [32768, 1], P('rows'), may hold values from 0 to 1023; in each aligned block of 1024 rows (0 to 1023, 1024 to 2047, ...) at most 2 rows name the same one
- age_rate: float32 [1024, 4], P('rows'), may hold values from 8 to 40
- kind_rate: float32 [1024, 8], P('rows'), may hold values from 2 to 20
Outputs:
- raked: float32 [32768, 2560], P('rows', 'rep')
- spread: float32 [32768, 32], P('rows')
The draws below stay inside these ranges and needn't reach their ends.
Inputs may be any that keep to these rules, and one draw needn't show every extreme that they name: `group_sizes`: each shard's 1024 sizes sum to 65536. `group_county`: among the 1024 block groups of one shard, no county holds more than 2.
All inputs are finite; a program needn't handle non-finite values.
Results may differ from the reference program's by a relative error of at most 0.0003.
Values sent between devices are 32-bit elements; how exact they have to be, the bound alone decides.
No kernel may reach another device: no remote copies, remote signals or barrier semaphores. Data moves between devices by JAX's collectives and lax.ppermute only.
A program may use at most 64 MiB of HBM per device.

```python
import math
import jax
import jax.numpy as jnp
import numpy as np
from jax import lax

REPS = 80
AGES = 4
KINDS = 8
CELLS = 32
LOW = 32
HIGH = 96
ITERS = 4
BG_DEV = 1024
SHARDS = 32
BGROUPS = 32768
RECORDS = 2097152
COUNTIES = 1024
PAIR = 2


def draw_cell_ids(key, part):
    key_perm, key_base, key_pick = jax.random.split(key, 3)
    kind_order = jax.random.permutation(key_perm, KINDS).astype(jnp.int32)
    tied_age = kind_order % AGES
    age_range = jnp.arange(AGES, dtype=jnp.int32)
    tied = (tied_age[None, :] == age_range[:, None]).astype(jnp.int32)
    base = jax.random.randint(key_base, (AGES, KINDS), 1, 4).astype(jnp.int32)
    cell_weight = (base + 24 * tied).reshape(-1)
    cumulative = jnp.cumsum(cell_weight).astype(jnp.int32)
    total = cumulative[-1]
    picks = jax.random.randint(key_pick, (RECORDS,), 0, total).astype(jnp.int32)
    return jnp.searchsorted(cumulative, picks, side='right').astype(jnp.int32)


def draw_group_sizes(key, part):
    key_a, key_b = jax.random.split(key)
    half_span = (HIGH - LOW) // 2
    middle = (HIGH + LOW) // 2
    raised = jax.random.randint(key_a, (SHARDS, BG_DEV), 0, half_span + 1)
    offset = jax.random.randint(key_b, (SHARDS, 1), 1, BG_DEV)
    column = jnp.arange(BG_DEV, dtype=jnp.int32)[None, :]
    raised = jnp.where(column == 0, half_span, raised)
    raised = jnp.where(column == offset, 0, raised)
    raised = jnp.where(column == BG_DEV - offset, 0, raised)
    partner = jnp.take_along_axis(raised, (column + offset) % BG_DEV, axis=1)
    return (middle + raised - partner).astype(jnp.int32)


def block_scale(own_key, shape, shards, least, largest):
    gain, own = 1.0, jax.random.fold_in(own_key, 6)
    for dim, shards_of in shards:
        heights = jnp.exp(jax.random.uniform(jax.random.fold_in(own, dim), (shards_of,), jnp.float32, least / len(shards), largest / len(shards)))
        gain = gain * jnp.repeat(heights, shape[dim] // shards_of).reshape([-1 if axis == dim else 1 for axis in range(len(shape))])
    return gain


def assign_block(key, own, number, rows, amount, top, reach, slope):
    sequence = jax.random.permutation(key, amount)
    heavy_load, ordinary = portions_of(amount, rows * top, reach, slope, True), portions_of(amount, rows * top, reach, slope, False)
    places = jnp.arange(amount)

    def named(tallies, rotation):
        used = int((tallies > 0).sum())
        fixed = max(1, used // 4)
        shifted = fixed + (places - fixed + rotation * (used - fixed)) % max(1, amount - fixed)
        return jnp.zeros((amount,), jnp.int32).at[sequence[jnp.where(places < fixed, places, shifted)]].set(jnp.asarray(tallies, jnp.int32))

    tallies = jnp.where(number % 4 == 0, named(heavy_load, number // 4), named(ordinary, number - number // 4 - 1))
    mixed = jax.random.permutation(jax.random.fold_in(own, 3), amount)
    giver, receiver = mixed[0:amount // 2 * 2:2], mixed[1:amount // 2 * 2:2]
    room = jnp.minimum(tallies[giver] - 1, reach - tallies[receiver]) // 2
    room = jnp.where((giver == sequence[0]) | (receiver == sequence[0]) | (tallies[receiver] == 0), 0, jnp.maximum(room, 0))
    shifted = jax.random.randint(jax.random.fold_in(own, 4), (amount // 2,), 0, 1 << 20) % (room + 1)
    tallies = tallies.at[giver].add(-shifted).at[receiver].add(shifted)
    labels = jnp.searchsorted(jnp.cumsum(tallies), jnp.arange(rows * top), side="right").astype(jnp.int32)
    listing = labels.reshape(top, rows).T
    listing = listing[jax.random.permutation(jax.random.fold_in(own, 1), rows)]
    rotation = jax.random.randint(jax.random.fold_in(own, 2), (rows, 1), 0, top)
    return jnp.take_along_axis(listing, (jnp.arange(top)[None, :] + rotation) % top, axis=1)


def portions_of(amount, total, bound, slope, full):
    weights = [(1 << 20) // math.isqrt(rank ** slope) + 1 for rank in range(1, amount + 1)]
    largest = bound if full else min(bound, max(-(-total // amount), total * weights[0] // sum(weights)))
    least = 1 if total - largest >= amount - 1 else 0
    holding, rest = [largest] + [least] * (amount - 1), total - largest - least * (amount - 1)
    while rest > 0:
        free = [i for i in range(1, amount) if holding[i] < largest] or [i for i in range(1, amount) if holding[i] < bound]
        mass, remaining = sum([weights[i] for i in free]), rest
        for i in free:
            extra = min(bound - holding[i], max(1, remaining * weights[i] // mass), rest)
            holding[i] = holding[i] + extra
            rest = rest - extra
    return np.array(holding)


def setup_inputs(seed: int = 0) -> dict:
    keys = jax.random.split(jax.random.key(seed), 7)
    weights = jnp.clip(jnp.exp(math.log(4.0) - 2.7725887 * jax.random.uniform(keys[0], (REPS, RECORDS), jnp.float32) ** block_scale(keys[0], (REPS, RECORDS), ((0, 4), (1, 32)), -0.2, 0.2)), 0.25, 4.0).astype(jnp.bfloat16)
    cell_ids = draw_cell_ids(jax.random.fold_in(keys[6], 71), 0)
    group_sizes = draw_group_sizes(jax.random.fold_in(keys[6], 71), 0)
    group_county_keys = jax.random.split(jax.random.fold_in(keys[3], 1), BGROUPS // BG_DEV)
    group_county_turns = jax.random.permutation(jax.random.fold_in(keys[3], 3), BGROUPS // BG_DEV)
    group_county = jax.vmap(lambda own, number: assign_block(jax.random.fold_in(keys[3], 2), own, number, BG_DEV, COUNTIES, 1, PAIR, 1))(group_county_keys, group_county_turns).reshape((BGROUPS, 1))
    age_rate = jnp.clip(jnp.exp(math.log(40.0) - 1.609438 * jax.random.uniform(keys[4], (COUNTIES, AGES), jnp.float32) ** block_scale(keys[4], (COUNTIES, AGES), ((0, 32),), -0.2, 0.2)), 8.0, 40.0)
    kind_rate = jnp.clip(jnp.exp(math.log(20.0) - 2.3025851 * jax.random.uniform(keys[5], (COUNTIES, KINDS), jnp.float32) ** block_scale(keys[5], (COUNTIES, KINDS), ((0, 32),), -0.2, 0.2)), 2.0, 20.0)
    return dict(weights=weights, cell_ids=cell_ids, group_sizes=group_sizes, group_county=group_county, age_rate=age_rate, kind_rate=kind_rate)


def rake(county_tables, groups_in, age_rate, kind_rate):
    county_rows = county_tables.shape[0]
    current = county_tables.reshape(county_rows, -1, AGES, KINDS)
    age_goal = (age_rate * groups_in[:, None])[:, None, :]
    kind_goal = (kind_rate * groups_in[:, None])[:, None, :]
    factor = jnp.ones_like(current)
    for sweep_index in range(ITERS):
        ratios = age_goal / jnp.maximum(jnp.sum(current, axis=3), 1.0)
        current = current * ratios[:, :, :, None]
        factor = factor * ratios[:, :, :, None]
        ratios = kind_goal / jnp.maximum(jnp.sum(current, axis=2), 1.0)
        current = current * ratios[:, :, None, :]
        factor = factor * ratios[:, :, None, :]
    return factor.reshape(county_rows, -1)


def reference(weights, cell_ids, group_sizes, group_county, age_rate, kind_rate):
    sizes_flat = group_sizes.reshape(-1)
    group_of = jnp.repeat(jnp.arange(BGROUPS, dtype=jnp.int32), sizes_flat, total_repeat_length=RECORDS).astype(jnp.int32)
    segment_ids = group_of * CELLS + cell_ids

    def per_replicate(weight_row):
        return jax.ops.segment_sum(weight_row.astype(jnp.float32), segment_ids, num_segments=BGROUPS * CELLS)

    per_rep = lax.map(per_replicate, weights)
    tables = per_rep.reshape(REPS, BGROUPS, CELLS).transpose(1, 0, 2).reshape(BGROUPS, REPS * CELLS)
    county_ids = group_county[:, 0]
    county_tables = jax.ops.segment_sum(tables, county_ids, num_segments=COUNTIES)
    groups_in = jax.ops.segment_sum(jnp.ones((BGROUPS,), jnp.float32), county_ids, num_segments=COUNTIES)
    factor = rake(county_tables, groups_in, age_rate, kind_rate)
    raked = tables * factor[county_ids]
    shaped = raked.reshape(BGROUPS, REPS, CELLS)
    centre = jnp.sum(shaped, axis=1) / REPS
    spread = jnp.sum(jnp.square(shaped - centre[:, None, :]), axis=1) * (4.0 / REPS)
    return raked, spread
```

```python
import jax
import jax.numpy as jnp
from jax import lax
from jax.experimental import pallas as pl
from jax.experimental.pallas import tpu as pltpu
from jax.sharding import PartitionSpec as P

AGES = 4
KINDS = 8
CELLS = 32
LOW = 32
ITERS = 4
BLOCK = 128
SPAN = 8
USE_KERNEL = True


def tab_kernel(offs_ref, seg_ref, w_ref, out_ref):
    steps = seg_ref.shape[0]
    width = SPAN * CELLS
    out_ref[...] = jnp.zeros_like(out_ref)
    rows = lax.broadcasted_iota(jnp.int32, (width, BLOCK), 0)

    def body(b, carry):
        seg = seg_ref[pl.ds(b, 1), :]
        hot = (rows == seg).astype(jnp.bfloat16)
        start = pl.multiple_of(b * BLOCK, BLOCK)
        w = w_ref[:, pl.ds(start, BLOCK)]
        part = lax.dot_general(
            w, hot, (((1,), (1,)), ((), ())), preferred_element_type=jnp.float32
        )
        off = pl.multiple_of(offs_ref[b], 128)
        out_ref[:, pl.ds(off, width)] += part
        return carry

    lax.fori_loop(0, steps, body, 0, unroll=8)


def tab_plain(offs, seg, weights, out_width):
    reps = weights.shape[0]
    steps = seg.shape[0]
    width = SPAN * CELLS
    hot = (seg[:, None, :] == jnp.arange(width, dtype=jnp.int32)[None, :, None])
    w = weights.reshape(reps, steps, BLOCK)
    part = jnp.einsum("rbi,bni->brn", w.astype(jnp.float32), hot.astype(jnp.float32),
                      precision=lax.Precision.HIGHEST)
    cols = offs[:, None] + jnp.arange(width, dtype=jnp.int32)[None, :]
    out = jnp.zeros((reps, out_width), jnp.float32)
    return out.at[:, cols.reshape(-1)].add(part.transpose(1, 0, 2).reshape(reps, -1))


def tabulate(weights, cell_ids, group_sizes):
    reps, records = weights.shape
    sizes = group_sizes[0]
    groups = sizes.shape[0]
    ends = jnp.cumsum(sizes).astype(jnp.int32)
    steps = records // BLOCK
    block_start = jnp.arange(steps, dtype=jnp.int32) * BLOCK
    first = jnp.sum((ends[None, :] <= block_start[:, None]).astype(jnp.int32), axis=1)
    base = first - first % 4
    ends_pad = jnp.concatenate([ends, jnp.full((SPAN,), records + 1, jnp.int32)])
    window = ends_pad[base[:, None] + jnp.arange(SPAN - 1, dtype=jnp.int32)[None, :]]
    place = block_start[:, None] + jnp.arange(BLOCK, dtype=jnp.int32)[None, :]
    local = jnp.zeros((steps, BLOCK), jnp.int32)
    for j in range(SPAN - 1):
        local = local + (window[:, j:j + 1] <= place).astype(jnp.int32)
    seg = local * CELLS + cell_ids.reshape(steps, BLOCK)
    offs = (base * CELLS).astype(jnp.int32)
    out_width = (groups + SPAN) * CELLS
    if USE_KERNEL:
        out = pl.pallas_call(
            tab_kernel,
            out_shape=jax.ShapeDtypeStruct((reps, out_width), jnp.float32),
            in_specs=[
                pl.BlockSpec(memory_space=pltpu.SMEM),
                pl.BlockSpec(memory_space=pltpu.VMEM),
                pl.BlockSpec(memory_space=pltpu.VMEM),
            ],
            out_specs=pl.BlockSpec(memory_space=pltpu.VMEM),
            cost_estimate=pl.CostEstimate(
                flops=2 * reps * records * SPAN * CELLS,
                bytes_accessed=weights.size * 2 + seg.size * 4 + reps * out_width * 4,
                transcendentals=0,
            ),
        )(offs, seg, weights)
    else:
        out = tab_plain(offs, seg, weights, out_width)
    out = out[:, :groups * CELLS].reshape(reps, groups, CELLS)
    return out.transpose(1, 0, 2).reshape(groups, reps * CELLS)


def rake_all(county_tables, groups_in, age_rate, kind_rate):
    counties, width = county_tables.shape
    reps = width // CELLS
    span = counties * reps
    current = county_tables.reshape(counties, reps, CELLS).transpose(2, 0, 1)
    current = current.reshape(AGES, KINDS, span)
    age_goal = (age_rate * groups_in[:, None]).T
    age_goal = jnp.broadcast_to(age_goal[:, :, None], (AGES, counties, reps)).reshape(AGES, span)
    kind_goal = (kind_rate * groups_in[:, None]).T
    kind_goal = jnp.broadcast_to(kind_goal[:, :, None], (KINDS, counties, reps)).reshape(KINDS, span)
    factor = jnp.ones_like(current)
    for sweep_index in range(ITERS):
        ratios = age_goal / jnp.maximum(jnp.sum(current, axis=1), 1.0)
        current = current * ratios[:, None, :]
        factor = factor * ratios[:, None, :]
        ratios = kind_goal / jnp.maximum(jnp.sum(current, axis=0), 1.0)
        current = current * ratios[None, :, :]
        factor = factor * ratios[None, :, :]
    factor = factor.reshape(CELLS, counties, reps).transpose(1, 2, 0)
    return factor.reshape(counties, width)


def local(weights, cell_ids, group_sizes, group_county, age_rate, kind_rate):
    rates = lax.all_gather(jnp.concatenate([age_rate, kind_rate], axis=1), "rows", tiled=True)
    tables = tabulate(weights, cell_ids, group_sizes)
    groups, width = tables.shape
    reps = width // CELLS
    county = group_county[:, 0]
    counties = rates.shape[0]
    group_range = jnp.arange(groups, dtype=jnp.int32)
    same = county[:, None] == county[None, :]
    earlier = group_range[:, None] > group_range[None, :]
    second = jnp.any(same & earlier, axis=1)
    county_range = jnp.arange(counties, dtype=jnp.int32)
    hits = county[None, :] == county_range[:, None]
    first_hit = hits & ~second[None, :]
    second_hit = hits & second[None, :]
    pick1 = jnp.where(jnp.any(first_hit, axis=1),
                      jnp.sum(jnp.where(first_hit, group_range[None, :], 0), axis=1), groups)
    pick2 = jnp.where(jnp.any(second_hit, axis=1),
                      jnp.sum(jnp.where(second_hit, group_range[None, :], 0), axis=1), groups)
    padded = jnp.concatenate([tables, jnp.zeros((1, width), tables.dtype)], axis=0)
    partial = jnp.take(padded, pick1, axis=0) + jnp.take(padded, pick2, axis=0)
    present = jnp.sum(hits.astype(jnp.float32), axis=1)
    county_tables, groups_in = lax.psum((partial, present), "rows")
    factor = rake_all(county_tables, groups_in, rates[:, :AGES], rates[:, AGES:])
    raked = tables * jnp.take(factor, county, axis=0)

    shaped = raked.reshape(groups, reps, CELLS)
    part_sum = jnp.sum(shaped, axis=1)
    part_mean = part_sum / reps
    part_m2 = jnp.sum(jnp.square(shaped - part_mean[:, None, :]), axis=1)
    stats = jnp.concatenate([part_sum, part_m2], axis=1)
    shards = lax.axis_size("rep")
    me = lax.axis_index("rep")
    received = [stats] + [
        lax.ppermute(stats, "rep", [(i, (i + s) % shards) for i in range(shards)])
        for s in range(1, shards)
    ]
    by_source = []
    for source in range(shards):
        value = jnp.zeros_like(stats)
        for s in range(shards):
            value = jnp.where((me - s) % shards == source, received[s], value)
        by_source.append(value)
    total_reps = reps * shards
    total = by_source[0][:, :CELLS]
    for source in range(1, shards):
        total = total + by_source[source][:, :CELLS]
    centre = total / total_reps
    deviation = None
    for source in range(shards):
        spread_in = by_source[source][:, CELLS:]
        gap = by_source[source][:, :CELLS] / reps - centre
        term = spread_in + reps * jnp.square(gap)
        deviation = term if deviation is None else deviation + term
    return (raked, deviation * (4.0 / total_reps))


def solution(mesh):
    placed = (
        P("rep", "rows"),
        P("rows"),
        P("rows", None),
        P("rows", None),
        P("rows", None),
        P("rows", None),
    )
    return jax.shard_map(
        local,
        mesh=mesh,
        in_specs=placed,
        out_specs=(P("rows", "rep"), P("rows", None)),
        check_vma=False,
    )
```

```python
import jax
import jax.numpy as jnp
from jax import lax
from jax.experimental import pallas as pl
from jax.experimental.pallas import tpu as pltpu
from jax.sharding import PartitionSpec as P

AGES = 4
KINDS = 8
CELLS = 32
LOW = 32
ITERS = 4
BLOCK = 128
SPAN = 8
USE_KERNEL = True


def tab_kernel(base_ref, ends_ref, cell_ref, w_ref, out_ref):
    steps = cell_ref.shape[0]
    width = SPAN * CELLS
    out_ref[...] = jnp.zeros_like(out_ref)
    rows = lax.broadcasted_iota(jnp.int32, (width, BLOCK), 0)
    lane = lax.broadcasted_iota(jnp.int32, (1, BLOCK), 1)

    def body(b, carry):
        first = base_ref[b]
        place = lane + b * BLOCK
        local = jnp.zeros((1, BLOCK), jnp.int32)
        for j in range(SPAN - 1):
            local = local + (place >= ends_ref[first + j]).astype(jnp.int32)
        seg = local * CELLS + cell_ref[pl.ds(b, 1), :]
        hot = (rows == seg).astype(jnp.bfloat16)
        start = pl.multiple_of(b * BLOCK, BLOCK)
        w = w_ref[:, pl.ds(start, BLOCK)]
        part = lax.dot_general(
            w, hot, (((1,), (1,)), ((), ())), preferred_element_type=jnp.float32
        )
        off = pl.multiple_of(first * CELLS, 128)
        out_ref[:, pl.ds(off, width)] += part
        return carry

    lax.fori_loop(0, steps, body, 0, unroll=4)


def tab_plain(base, ends_pad, cells, weights, out_width):
    reps = weights.shape[0]
    steps = cells.shape[0]
    width = SPAN * CELLS
    window = ends_pad[base[:, None] + jnp.arange(SPAN - 1, dtype=jnp.int32)[None, :]]
    place = (jnp.arange(steps, dtype=jnp.int32) * BLOCK)[:, None] + jnp.arange(BLOCK, dtype=jnp.int32)[None, :]
    local = jnp.zeros((steps, BLOCK), jnp.int32)
    for j in range(SPAN - 1):
        local = local + (place >= window[:, j:j + 1]).astype(jnp.int32)
    seg = local * CELLS + cells
    hot = (seg[:, None, :] == jnp.arange(width, dtype=jnp.int32)[None, :, None])
    w = weights.reshape(reps, steps, BLOCK)
    part = jnp.einsum("rbi,bni->brn", w.astype(jnp.float32), hot.astype(jnp.float32),
                      precision=lax.Precision.HIGHEST)
    cols = (base * CELLS)[:, None] + jnp.arange(width, dtype=jnp.int32)[None, :]
    out = jnp.zeros((reps, out_width), jnp.float32)
    return out.at[:, cols.reshape(-1)].add(part.transpose(1, 0, 2).reshape(reps, -1))


def tabulate(weights, cell_ids, group_sizes):
    reps, records = weights.shape
    sizes = group_sizes[0]
    groups = sizes.shape[0]
    ends = jnp.cumsum(sizes).astype(jnp.int32)
    steps = records // BLOCK
    block_start = jnp.arange(steps, dtype=jnp.int32) * BLOCK
    first = jnp.sum((ends[None, :] <= block_start[:, None]).astype(jnp.int32), axis=1)
    base = (first - first % 4).astype(jnp.int32)
    ends_pad = jnp.concatenate([ends, jnp.full((SPAN,), records + 1, jnp.int32)])
    cells = cell_ids.reshape(steps, BLOCK)
    out_width = (groups + SPAN) * CELLS
    if USE_KERNEL:
        out = pl.pallas_call(
            tab_kernel,
            out_shape=jax.ShapeDtypeStruct((reps, out_width), jnp.float32),
            in_specs=[
                pl.BlockSpec(memory_space=pltpu.SMEM),
                pl.BlockSpec(memory_space=pltpu.SMEM),
                pl.BlockSpec(memory_space=pltpu.VMEM),
                pl.BlockSpec(memory_space=pltpu.VMEM),
            ],
            out_specs=pl.BlockSpec(memory_space=pltpu.VMEM),
            cost_estimate=pl.CostEstimate(
                flops=2 * reps * records * SPAN * CELLS,
                bytes_accessed=weights.size * 2 + cells.size * 4 + reps * out_width * 4,
                transcendentals=0,
            ),
        )(base, ends_pad, cells, weights)
    else:
        out = tab_plain(base, ends_pad, cells, weights, out_width)
    out = out[:, :groups * CELLS].reshape(reps, groups, CELLS)
    return out.transpose(1, 0, 2).reshape(groups, reps * CELLS)


def exact_dot(left, right):
    return jnp.dot(left, right, precision=lax.Precision.HIGHEST, preferred_element_type=jnp.float32)


def rake_own(county_tables, groups_in, age_rate, kind_rate):
    counties, width = county_tables.shape
    reps = width // CELLS
    span = counties * reps
    current = county_tables.reshape(counties, reps, CELLS).transpose(2, 0, 1)
    current = current.reshape(AGES, KINDS, span)
    age_goal = (age_rate * groups_in[:, None]).T
    age_goal = jnp.broadcast_to(age_goal[:, :, None], (AGES, counties, reps)).reshape(AGES, span)
    kind_goal = (kind_rate * groups_in[:, None]).T
    kind_goal = jnp.broadcast_to(kind_goal[:, :, None], (KINDS, counties, reps)).reshape(KINDS, span)
    age_factor = jnp.ones((AGES, span), jnp.float32)
    kind_factor = jnp.ones((KINDS, span), jnp.float32)
    for sweep_index in range(ITERS):
        ratios = age_goal / jnp.maximum(jnp.sum(current, axis=1), 1.0)
        current = current * ratios[:, None, :]
        age_factor = age_factor * ratios
        ratios = kind_goal / jnp.maximum(jnp.sum(current, axis=0), 1.0)
        current = current * ratios[None, :, :]
        kind_factor = kind_factor * ratios
    age_factor = age_factor.reshape(AGES, counties, reps).transpose(1, 2, 0).reshape(counties, reps * AGES)
    kind_factor = kind_factor.reshape(KINDS, counties, reps).transpose(1, 2, 0).reshape(counties, reps * KINDS)
    return jnp.concatenate([age_factor, kind_factor], axis=1)


def spreaders(reps):
    col = jnp.arange(reps * CELLS, dtype=jnp.int32)
    rep_of, cell_of = col // CELLS, col % CELLS
    age_row = jnp.arange(reps * AGES, dtype=jnp.int32)
    kind_row = jnp.arange(reps * KINDS, dtype=jnp.int32)
    to_age = ((age_row[:, None] // AGES == rep_of[None, :])
              & (age_row[:, None] % AGES == cell_of[None, :] // KINDS)).astype(jnp.float32)
    to_kind = ((kind_row[:, None] // KINDS == rep_of[None, :])
               & (kind_row[:, None] % KINDS == cell_of[None, :] % KINDS)).astype(jnp.float32)
    cell_sum = (cell_of[:, None] == jnp.arange(CELLS, dtype=jnp.int32)[None, :]).astype(jnp.float32)
    return to_age, to_kind, cell_sum


def local(weights, cell_ids, group_sizes, group_county, age_rate, kind_rate):
    tables = tabulate(weights, cell_ids, group_sizes)
    groups, width = tables.shape
    reps = width // CELLS
    county = group_county[:, 0]
    owners = lax.axis_size("rows")
    county_here = age_rate.shape[0]
    counties = county_here * owners
    group_range = jnp.arange(groups, dtype=jnp.int32)
    same = county[:, None] == county[None, :]
    earlier = group_range[:, None] > group_range[None, :]
    second = jnp.any(same & earlier, axis=1)
    county_range = jnp.arange(counties, dtype=jnp.int32)
    hits = county[None, :] == county_range[:, None]
    first_hit = hits & ~second[None, :]
    second_hit = hits & second[None, :]
    pick1 = jnp.where(jnp.any(first_hit, axis=1),
                      jnp.sum(jnp.where(first_hit, group_range[None, :], 0), axis=1), groups)
    pick2 = jnp.where(jnp.any(second_hit, axis=1),
                      jnp.sum(jnp.where(second_hit, group_range[None, :], 0), axis=1), groups)
    padded = jnp.concatenate([tables, jnp.zeros((1, width), tables.dtype)], axis=0)
    partial = jnp.take(padded, pick1, axis=0) + jnp.take(padded, pick2, axis=0)
    present = jnp.sum(hits.astype(jnp.float32), axis=1).reshape(owners, 1, county_here)
    present = jnp.pad(present, ((0, 0), (0, 0), (0, width - county_here)))
    outgoing = jnp.concatenate([partial.reshape(owners, county_here, width), present], axis=1)
    arrived = lax.all_to_all(
        outgoing.reshape(owners * (county_here + 1), width), "rows", 0, 0, tiled=True
    ).reshape(owners, county_here + 1, width)
    summed = jnp.sum(arrived, axis=0)
    county_tables = summed[:county_here]
    groups_in = summed[county_here, :county_here]
    factors = rake_own(county_tables, groups_in, age_rate, kind_rate)
    factors = lax.all_gather(factors, "rows", tiled=True)
    mine = jnp.take(factors, county, axis=0)
    to_age, to_kind, cell_sum = spreaders(reps)
    factor = exact_dot(mine[:, :reps * AGES], to_age) * exact_dot(mine[:, reps * AGES:], to_kind)
    raked = tables * factor

    part_sum = exact_dot(raked, cell_sum)
    part_mean = part_sum / reps
    gap = raked - exact_dot(part_mean, cell_sum.T)
    part_m2 = exact_dot(jnp.square(gap), cell_sum)
    stats = jnp.concatenate([part_sum, part_m2], axis=1)
    shards = lax.axis_size("rep")
    me = lax.axis_index("rep")
    received = [stats] + [
        lax.ppermute(stats, "rep", [(i, (i + s) % shards) for i in range(shards)])
        for s in range(1, shards)
    ]
    by_source = []
    for source in range(shards):
        value = jnp.zeros_like(stats)
        for s in range(shards):
            value = jnp.where((me - s) % shards == source, received[s], value)
        by_source.append(value)
    total_reps = reps * shards
    total = by_source[0][:, :CELLS]
    for source in range(1, shards):
        total = total + by_source[source][:, :CELLS]
    centre = total / total_reps
    deviation = None
    for source in range(shards):
        spread_in = by_source[source][:, CELLS:]
        off_centre = by_source[source][:, :CELLS] / reps - centre
        term = spread_in + reps * jnp.square(off_centre)
        deviation = term if deviation is None else deviation + term
    return (raked, deviation * (4.0 / total_reps))


def solution(mesh):
    placed = (
        P("rep", "rows"),
        P("rows"),
        P("rows", None),
        P("rows", None),
        P("rows", None),
        P("rows", None),
    )
    return jax.shard_map(
        local,
        mesh=mesh,
        in_specs=placed,
        out_specs=(P("rows", "rep"), P("rows", None)),
        check_vma=False,
    )
```

```python
import jax
import jax.numpy as jnp
from jax import lax
from jax.experimental import pallas as pl
from jax.experimental.pallas import tpu as pltpu
from jax.sharding import PartitionSpec as P

AGES = 4
KINDS = 8
CELLS = 32
LOW = 32
ITERS = 4
BLOCK = 128
SPAN = 8
USE_KERNEL = True


def tab_kernel(offs_ref, seg_ref, w_ref, out_ref):
    steps = seg_ref.shape[0]
    width = SPAN * CELLS
    out_ref[...] = jnp.zeros_like(out_ref)
    rows = lax.broadcasted_iota(jnp.int32, (width, BLOCK), 0)

    def body(b, carry):
        seg = seg_ref[pl.ds(b, 1), :]
        hot = (rows == seg).astype(jnp.bfloat16)
        start = pl.multiple_of(b * BLOCK, BLOCK)
        w = w_ref[:, pl.ds(start, BLOCK)]
        part = lax.dot_general(
            w, hot, (((1,), (1,)), ((), ())), preferred_element_type=jnp.float32
        )
        off = pl.multiple_of(offs_ref[b], 128)
        out_ref[:, pl.ds(off, width)] += part
        return carry

    lax.fori_loop(0, steps, body, 0, unroll=4)


def tab_plain(offs, seg, weights, out_width):
    reps = weights.shape[0]
    steps = seg.shape[0]
    width = SPAN * CELLS
    hot = (seg[:, None, :] == jnp.arange(width, dtype=jnp.int32)[None, :, None])
    w = weights.reshape(reps, steps, BLOCK)
    part = jnp.einsum("rbi,bni->brn", w.astype(jnp.float32), hot.astype(jnp.float32),
                      precision=lax.Precision.HIGHEST)
    cols = offs[:, None] + jnp.arange(width, dtype=jnp.int32)[None, :]
    out = jnp.zeros((reps, out_width), jnp.float32)
    return out.at[:, cols.reshape(-1)].add(part.transpose(1, 0, 2).reshape(reps, -1))


def tabulate(weights, cell_ids, group_sizes):
    reps, records = weights.shape
    sizes = group_sizes[0]
    groups = sizes.shape[0]
    ends = jnp.cumsum(sizes).astype(jnp.int32)
    steps = records // BLOCK
    block_start = jnp.arange(steps, dtype=jnp.int32) * BLOCK
    first = jnp.sum((ends[None, :] <= block_start[:, None]).astype(jnp.int32), axis=1)
    base = (first - first % 4).astype(jnp.int32)
    group_range = jnp.arange(groups, dtype=jnp.int32)
    place = block_start[:, None] + jnp.arange(BLOCK, dtype=jnp.int32)[None, :]
    local = jnp.zeros((steps, BLOCK), jnp.int32)
    for j in range(SPAN - 1):
        chosen = group_range[None, :] == (base + j)[:, None]
        edge = jnp.sum(jnp.where(chosen, ends[None, :], 0), axis=1)
        edge = jnp.where(base + j < groups, edge, records + 1)
        local = local + (place >= edge[:, None]).astype(jnp.int32)
    seg = local * CELLS + cell_ids.reshape(steps, BLOCK)
    offs = (base * CELLS).astype(jnp.int32)
    out_width = (groups + SPAN) * CELLS
    if USE_KERNEL:
        out = pl.pallas_call(
            tab_kernel,
            out_shape=jax.ShapeDtypeStruct((reps, out_width), jnp.float32),
            in_specs=[
                pl.BlockSpec(memory_space=pltpu.SMEM),
                pl.BlockSpec(memory_space=pltpu.VMEM),
                pl.BlockSpec(memory_space=pltpu.VMEM),
            ],
            out_specs=pl.BlockSpec(memory_space=pltpu.VMEM),
            cost_estimate=pl.CostEstimate(
                flops=2 * reps * records * SPAN * CELLS,
                bytes_accessed=weights.size * 2 + seg.size * 4 + reps * out_width * 4,
                transcendentals=0,
            ),
        )(offs, seg, weights)
    else:
        out = tab_plain(offs, seg, weights, out_width)
    out = out[:, :groups * CELLS].reshape(reps, groups, CELLS)
    return out.transpose(1, 0, 2).reshape(groups, reps * CELLS)


def exact_dot(left, right):
    return jnp.dot(left, right, precision=lax.Precision.HIGHEST, preferred_element_type=jnp.float32)


def rake_own(county_tables, groups_in, age_rate, kind_rate):
    counties, width = county_tables.shape
    reps = width // CELLS
    span = counties * reps
    current = county_tables.reshape(counties, reps, CELLS).transpose(2, 0, 1)
    current = current.reshape(AGES, KINDS, span)
    age_goal = (age_rate * groups_in[:, None]).T
    age_goal = jnp.broadcast_to(age_goal[:, :, None], (AGES, counties, reps)).reshape(AGES, span)
    kind_goal = (kind_rate * groups_in[:, None]).T
    kind_goal = jnp.broadcast_to(kind_goal[:, :, None], (KINDS, counties, reps)).reshape(KINDS, span)
    age_factor = jnp.ones((AGES, span), jnp.float32)
    kind_factor = jnp.ones((KINDS, span), jnp.float32)
    for sweep_index in range(ITERS):
        ratios = age_goal / jnp.maximum(jnp.sum(current, axis=1), 1.0)
        current = current * ratios[:, None, :]
        age_factor = age_factor * ratios
        ratios = kind_goal / jnp.maximum(jnp.sum(current, axis=0), 1.0)
        current = current * ratios[None, :, :]
        kind_factor = kind_factor * ratios
    age_factor = age_factor.reshape(AGES, counties, reps).transpose(1, 2, 0).reshape(counties, reps * AGES)
    kind_factor = kind_factor.reshape(KINDS, counties, reps).transpose(1, 2, 0).reshape(counties, reps * KINDS)
    return jnp.concatenate([age_factor, kind_factor], axis=1)


def spreaders(reps):
    col = jnp.arange(reps * CELLS, dtype=jnp.int32)
    rep_of, cell_of = col // CELLS, col % CELLS
    age_row = jnp.arange(reps * AGES, dtype=jnp.int32)
    kind_row = jnp.arange(reps * KINDS, dtype=jnp.int32)
    to_age = ((age_row[:, None] // AGES == rep_of[None, :])
              & (age_row[:, None] % AGES == cell_of[None, :] // KINDS)).astype(jnp.float32)
    to_kind = ((kind_row[:, None] // KINDS == rep_of[None, :])
               & (kind_row[:, None] % KINDS == cell_of[None, :] % KINDS)).astype(jnp.float32)
    cell_sum = (cell_of[:, None] == jnp.arange(CELLS, dtype=jnp.int32)[None, :]).astype(jnp.float32)
    return to_age, to_kind, cell_sum


def local(weights, cell_ids, group_sizes, group_county, age_rate, kind_rate):
    tables = tabulate(weights, cell_ids, group_sizes)
    groups, width = tables.shape
    reps = width // CELLS
    county = group_county[:, 0]
    owners = lax.axis_size("rows")
    county_here = age_rate.shape[0]
    counties = county_here * owners
    county_range = jnp.arange(counties, dtype=jnp.int32)
    hits = county[None, :] == county_range[:, None]
    partial = exact_dot(hits.astype(jnp.float32), tables)
    present = jnp.sum(hits.astype(jnp.float32), axis=1).reshape(owners, 1, county_here)
    present = jnp.pad(present, ((0, 0), (0, 0), (0, width - county_here)))
    outgoing = jnp.concatenate([partial.reshape(owners, county_here, width), present], axis=1)
    arrived = lax.all_to_all(
        outgoing.reshape(owners * (county_here + 1), width), "rows", 0, 0, tiled=True
    ).reshape(owners, county_here + 1, width)
    summed = jnp.sum(arrived, axis=0)
    county_tables = summed[:county_here]
    groups_in = summed[county_here, :county_here]
    factors = rake_own(county_tables, groups_in, age_rate, kind_rate)
    factors = lax.all_gather(factors, "rows", tiled=True)
    mine = jnp.take(factors, county, axis=0)
    to_age, to_kind, cell_sum = spreaders(reps)
    factor = exact_dot(mine[:, :reps * AGES], to_age) * exact_dot(mine[:, reps * AGES:], to_kind)
    raked = tables * factor

    part_sum = exact_dot(raked, cell_sum)
    part_mean = part_sum / reps
    gap = raked - exact_dot(part_mean, cell_sum.T)
    part_m2 = exact_dot(jnp.square(gap), cell_sum)
    stats = jnp.concatenate([part_sum, part_m2], axis=1)
    shards = lax.axis_size("rep")
    me = lax.axis_index("rep")
    received = [stats] + [
        lax.ppermute(stats, "rep", [(i, (i + s) % shards) for i in range(shards)])
        for s in range(1, shards)
    ]
    by_source = []
    for source in range(shards):
        value = jnp.zeros_like(stats)
        for s in range(shards):
            value = jnp.where((me - s) % shards == source, received[s], value)
        by_source.append(value)
    total_reps = reps * shards
    total = by_source[0][:, :CELLS]
    for source in range(1, shards):
        total = total + by_source[source][:, :CELLS]
    centre = total / total_reps
    deviation = None
    for source in range(shards):
        spread_in = by_source[source][:, CELLS:]
        off_centre = by_source[source][:, :CELLS] / reps - centre
        term = spread_in + reps * jnp.square(off_centre)
        deviation = term if deviation is None else deviation + term
    return (raked, deviation * (4.0 / total_reps))


def solution(mesh):
    placed = (
        P("rep", "rows"),
        P("rows"),
        P("rows", None),
        P("rows", None),
        P("rows", None),
        P("rows", None),
    )
    return jax.shard_map(
        local,
        mesh=mesh,
        in_specs=placed,
        out_specs=(P("rows", "rep"), P("rows", None)),
        check_vma=False,
    )
```

```python
import jax
import jax.numpy as jnp
from jax import lax
from jax.experimental import pallas as pl
from jax.experimental.pallas import tpu as pltpu
from jax.sharding import PartitionSpec as P

AGES = 4
KINDS = 8
CELLS = 32
LOW = 32
ITERS = 4
BLOCK = 128
SPAN = 8
USE_KERNEL = True


def tab_kernel(offs_ref, seg_ref, w_ref, out_ref):
    steps = seg_ref.shape[0]
    width = SPAN * CELLS
    out_ref[...] = jnp.zeros_like(out_ref)
    rows = lax.broadcasted_iota(jnp.int32, (width, BLOCK), 0)

    def body(b, carry):
        seg = seg_ref[pl.ds(b, 1), :]
        hot = (rows == seg).astype(jnp.bfloat16)
        start = pl.multiple_of(b * BLOCK, BLOCK)
        w = w_ref[:, pl.ds(start, BLOCK)]
        part = lax.dot_general(
            w, hot, (((1,), (1,)), ((), ())), preferred_element_type=jnp.float32
        )
        off = pl.multiple_of(offs_ref[b], 128)
        out_ref[:, pl.ds(off, width)] += part
        return carry

    lax.fori_loop(0, steps, body, 0, unroll=8)


def tab_plain(offs, seg, weights, out_width):
    reps = weights.shape[0]
    steps = seg.shape[0]
    width = SPAN * CELLS
    hot = (seg[:, None, :] == jnp.arange(width, dtype=jnp.int32)[None, :, None])
    w = weights.reshape(reps, steps, BLOCK)
    part = jnp.einsum("rbi,bni->brn", w.astype(jnp.float32), hot.astype(jnp.float32),
                      precision=lax.Precision.HIGHEST)
    cols = offs[:, None] + jnp.arange(width, dtype=jnp.int32)[None, :]
    out = jnp.zeros((reps, out_width), jnp.float32)
    return out.at[:, cols.reshape(-1)].add(part.transpose(1, 0, 2).reshape(reps, -1))


def tabulate(weights, cell_ids, group_sizes):
    reps, records = weights.shape
    sizes = group_sizes[0]
    groups = sizes.shape[0]
    ends = jnp.cumsum(sizes).astype(jnp.int32)
    steps = records // BLOCK
    block_start = jnp.arange(steps, dtype=jnp.int32) * BLOCK
    first = jnp.sum((ends[None, :] <= block_start[:, None]).astype(jnp.int32), axis=1)
    base = jnp.minimum(first - first % 4, groups - SPAN).astype(jnp.int32)
    group_range = jnp.arange(groups, dtype=jnp.int32)
    place = block_start[:, None] + jnp.arange(BLOCK, dtype=jnp.int32)[None, :]
    local = jnp.zeros((steps, BLOCK), jnp.int32)
    for j in range(SPAN - 1):
        chosen = group_range[None, :] == (base + j)[:, None]
        edge = jnp.sum(jnp.where(chosen, ends[None, :], 0), axis=1)
        edge = jnp.where(base + j < groups, edge, records + 1)
        local = local + (place >= edge[:, None]).astype(jnp.int32)
    seg = local * CELLS + cell_ids.reshape(steps, BLOCK)
    offs = (base * CELLS).astype(jnp.int32)
    out_width = groups * CELLS
    if USE_KERNEL:
        out = pl.pallas_call(
            tab_kernel,
            out_shape=jax.ShapeDtypeStruct((reps, out_width), jnp.float32),
            in_specs=[
                pl.BlockSpec(memory_space=pltpu.SMEM),
                pl.BlockSpec(memory_space=pltpu.VMEM),
                pl.BlockSpec(memory_space=pltpu.VMEM),
            ],
            out_specs=pl.BlockSpec(memory_space=pltpu.VMEM),
            cost_estimate=pl.CostEstimate(
                flops=2 * reps * records * SPAN * CELLS,
                bytes_accessed=weights.size * 2 + seg.size * 4 + reps * out_width * 4,
                transcendentals=0,
            ),
        )(offs, seg, weights)
    else:
        out = tab_plain(offs, seg, weights, out_width)
    out = out.reshape(reps, groups, CELLS)
    return out.transpose(1, 0, 2).reshape(groups, reps * CELLS)


def exact_dot(left, right):
    return jnp.dot(left, right, precision=lax.Precision.HIGHEST, preferred_element_type=jnp.float32)


def rake_own(county_tables, groups_in, age_rate, kind_rate):
    counties, width = county_tables.shape
    reps = width // CELLS
    span = counties * reps
    current = county_tables.reshape(counties, reps, CELLS).transpose(2, 0, 1)
    current = current.reshape(AGES, KINDS, span)
    age_goal = (age_rate * groups_in[:, None]).T
    age_goal = jnp.broadcast_to(age_goal[:, :, None], (AGES, counties, reps)).reshape(AGES, span)
    kind_goal = (kind_rate * groups_in[:, None]).T
    kind_goal = jnp.broadcast_to(kind_goal[:, :, None], (KINDS, counties, reps)).reshape(KINDS, span)
    age_factor = jnp.ones((AGES, span), jnp.float32)
    kind_factor = jnp.ones((KINDS, span), jnp.float32)
    for sweep_index in range(ITERS):
        ratios = age_goal / jnp.maximum(jnp.sum(current, axis=1), 1.0)
        current = current * ratios[:, None, :]
        age_factor = age_factor * ratios
        ratios = kind_goal / jnp.maximum(jnp.sum(current, axis=0), 1.0)
        current = current * ratios[None, :, :]
        kind_factor = kind_factor * ratios
    age_factor = age_factor.reshape(AGES, counties, reps).transpose(1, 2, 0).reshape(counties, reps * AGES)
    kind_factor = kind_factor.reshape(KINDS, counties, reps).transpose(1, 2, 0).reshape(counties, reps * KINDS)
    return jnp.concatenate([age_factor, kind_factor], axis=1)


def spreaders(reps):
    col = jnp.arange(reps * CELLS, dtype=jnp.int32)
    rep_of, cell_of = col // CELLS, col % CELLS
    age_row = jnp.arange(reps * AGES, dtype=jnp.int32)
    kind_row = jnp.arange(reps * KINDS, dtype=jnp.int32)
    to_age = ((age_row[:, None] // AGES == rep_of[None, :])
              & (age_row[:, None] % AGES == cell_of[None, :] // KINDS)).astype(jnp.float32)
    to_kind = ((kind_row[:, None] // KINDS == rep_of[None, :])
               & (kind_row[:, None] % KINDS == cell_of[None, :] % KINDS)).astype(jnp.float32)
    cell_sum = (cell_of[:, None] == jnp.arange(CELLS, dtype=jnp.int32)[None, :]).astype(jnp.float32)
    return to_age, to_kind, cell_sum


def local(weights, cell_ids, group_sizes, group_county, age_rate, kind_rate):
    tables = tabulate(weights, cell_ids, group_sizes)
    groups, width = tables.shape
    reps = width // CELLS
    county = group_county[:, 0]
    owners = lax.axis_size("rows")
    county_here = age_rate.shape[0]
    counties = county_here * owners
    county_range = jnp.arange(counties, dtype=jnp.int32)
    hits = county[None, :] == county_range[:, None]
    partial = exact_dot(hits.astype(jnp.float32), tables)
    present = jnp.sum(hits.astype(jnp.float32), axis=1).reshape(owners, 1, county_here)
    present = jnp.pad(present, ((0, 0), (0, 0), (0, width - county_here)))
    outgoing = jnp.concatenate([partial.reshape(owners, county_here, width), present], axis=1)
    arrived = lax.all_to_all(
        outgoing.reshape(owners * (county_here + 1), width), "rows", 0, 0, tiled=True
    ).reshape(owners, county_here + 1, width)
    summed = jnp.sum(arrived, axis=0)
    county_tables = summed[:county_here]
    groups_in = summed[county_here, :county_here]
    factors = rake_own(county_tables, groups_in, age_rate, kind_rate)
    sent = jnp.broadcast_to(factors[None], (owners,) + factors.shape)
    factors = lax.all_to_all(
        sent.reshape(owners * county_here, factors.shape[1]), "rows", 0, 0, tiled=True
    )
    mine = jnp.take(factors, county, axis=0)
    to_age, to_kind, cell_sum = spreaders(reps)
    factor = exact_dot(mine[:, :reps * AGES], to_age) * exact_dot(mine[:, reps * AGES:], to_kind)
    raked = tables * factor

    part_sum = exact_dot(raked, cell_sum)
    part_mean = part_sum / reps
    gap = raked - exact_dot(part_mean, cell_sum.T)
    part_m2 = exact_dot(jnp.square(gap), cell_sum)
    stats = jnp.concatenate([part_sum, part_m2], axis=1)
    shards = lax.axis_size("rep")
    me = lax.axis_index("rep")
    received = [stats] + [
        lax.ppermute(stats, "rep", [(i, (i + s) % shards) for i in range(shards)])
        for s in range(1, shards)
    ]
    by_source = []
    for source in range(shards):
        value = jnp.zeros_like(stats)
        for s in range(shards):
            value = jnp.where((me - s) % shards == source, received[s], value)
        by_source.append(value)
    total_reps = reps * shards
    total = by_source[0][:, :CELLS]
    for source in range(1, shards):
        total = total + by_source[source][:, :CELLS]
    centre = total / total_reps
    deviation = None
    for source in range(shards):
        spread_in = by_source[source][:, CELLS:]
        off_centre = by_source[source][:, :CELLS] / reps - centre
        term = spread_in + reps * jnp.square(off_centre)
        deviation = term if deviation is None else deviation + term
    return (raked, deviation * (4.0 / total_reps))


def solution(mesh):
    placed = (
        P("rep", "rows"),
        P("rows"),
        P("rows", None),
        P("rows", None),
        P("rows", None),
        P("rows", None),
    )
    return jax.shard_map(
        local,
        mesh=mesh,
        in_specs=placed,
        out_specs=(P("rows", "rep"), P("rows", None)),
        check_vma=False,
    )
```

```python
import jax
import jax.numpy as jnp
from jax import lax
from jax.experimental import pallas as pl
from jax.experimental.pallas import tpu as pltpu
from jax.sharding import PartitionSpec as P

AGES = 4
KINDS = 8
CELLS = 32
LOW = 32
ITERS = 4
BLOCK = 128
SPAN = 8
USE_KERNEL = True


def tab_kernel(offs_ref, seg_ref, w_ref, out_ref):
    steps = seg_ref.shape[0]
    width = SPAN * CELLS
    out_ref[...] = jnp.zeros_like(out_ref)
    rows = lax.broadcasted_iota(jnp.int32, (width, BLOCK), 0)

    def body(b, carry):
        seg = seg_ref[pl.ds(b, 1), :]
        hot = (rows == seg).astype(jnp.bfloat16)
        start = pl.multiple_of(b * BLOCK, BLOCK)
        w = w_ref[:, pl.ds(start, BLOCK)]
        part = lax.dot_general(
            w, hot, (((1,), (1,)), ((), ())), preferred_element_type=jnp.float32
        )
        off = pl.multiple_of(offs_ref[b], 128)
        out_ref[:, pl.ds(off, width)] += part
        return carry

    lax.fori_loop(0, steps, body, 0, unroll=8)


def tab_plain(offs, seg, weights, out_width):
    reps = weights.shape[0]
    steps = seg.shape[0]
    width = SPAN * CELLS
    hot = (seg[:, None, :] == jnp.arange(width, dtype=jnp.int32)[None, :, None])
    w = weights.reshape(reps, steps, BLOCK)
    part = jnp.einsum("rbi,bni->brn", w.astype(jnp.float32), hot.astype(jnp.float32),
                      precision=lax.Precision.HIGHEST)
    cols = offs[:, None] + jnp.arange(width, dtype=jnp.int32)[None, :]
    out = jnp.zeros((reps, out_width), jnp.float32)
    return out.at[:, cols.reshape(-1)].add(part.transpose(1, 0, 2).reshape(reps, -1))


def tabulate(weights, cell_ids, group_sizes):
    reps, records = weights.shape
    sizes = group_sizes[0]
    groups = sizes.shape[0]
    ends = jnp.cumsum(sizes).astype(jnp.int32)
    steps = records // BLOCK
    block_start = jnp.arange(steps, dtype=jnp.int32) * BLOCK
    first = jnp.sum((ends[None, :] <= block_start[:, None]).astype(jnp.int32), axis=1)
    base = jnp.minimum(first - first % 4, groups - SPAN).astype(jnp.int32)
    group_range = jnp.arange(groups, dtype=jnp.int32)
    place = block_start[:, None] + jnp.arange(BLOCK, dtype=jnp.int32)[None, :]
    local = jnp.zeros((steps, BLOCK), jnp.int32)
    for j in range(SPAN - 1):
        chosen = group_range[None, :] == (base + j)[:, None]
        edge = jnp.sum(jnp.where(chosen, ends[None, :], 0), axis=1)
        edge = jnp.where(base + j < groups, edge, records + 1)
        local = local + (place >= edge[:, None]).astype(jnp.int32)
    seg = local * CELLS + cell_ids.reshape(steps, BLOCK)
    offs = (base * CELLS).astype(jnp.int32)
    out_width = groups * CELLS
    if USE_KERNEL:
        out = pl.pallas_call(
            tab_kernel,
            out_shape=jax.ShapeDtypeStruct((reps, out_width), jnp.float32),
            in_specs=[
                pl.BlockSpec(memory_space=pltpu.SMEM),
                pl.BlockSpec(memory_space=pltpu.VMEM),
                pl.BlockSpec(memory_space=pltpu.VMEM),
            ],
            out_specs=pl.BlockSpec(memory_space=pltpu.VMEM),
            cost_estimate=pl.CostEstimate(
                flops=2 * reps * records * SPAN * CELLS,
                bytes_accessed=weights.size * 2 + seg.size * 4 + reps * out_width * 4,
                transcendentals=0,
            ),
        )(offs, seg, weights)
    else:
        out = tab_plain(offs, seg, weights, out_width)
    out = out.reshape(reps, groups, CELLS)
    return out.transpose(1, 0, 2).reshape(groups, reps * CELLS)


def exact_dot(left, right):
    return jnp.dot(left, right, precision=lax.Precision.HIGHEST, preferred_element_type=jnp.float32)


def rake_own(county_tables, groups_in, age_rate, kind_rate):
    counties, width = county_tables.shape
    reps = width // CELLS
    span = counties * reps
    current = county_tables.reshape(counties, reps, CELLS).transpose(2, 0, 1)
    current = current.reshape(AGES, KINDS, span)
    age_goal = (age_rate * groups_in[:, None]).T
    age_goal = jnp.broadcast_to(age_goal[:, :, None], (AGES, counties, reps)).reshape(AGES, span)
    kind_goal = (kind_rate * groups_in[:, None]).T
    kind_goal = jnp.broadcast_to(kind_goal[:, :, None], (KINDS, counties, reps)).reshape(KINDS, span)
    age_factor = jnp.ones((AGES, span), jnp.float32)
    kind_factor = jnp.ones((KINDS, span), jnp.float32)
    for sweep_index in range(ITERS):
        ratios = age_goal / jnp.maximum(jnp.sum(current, axis=1), 1.0)
        current = current * ratios[:, None, :]
        age_factor = age_factor * ratios
        ratios = kind_goal / jnp.maximum(jnp.sum(current, axis=0), 1.0)
        current = current * ratios[None, :, :]
        kind_factor = kind_factor * ratios
    age_factor = age_factor.reshape(AGES, counties, reps).transpose(1, 2, 0).reshape(counties, reps * AGES)
    kind_factor = kind_factor.reshape(KINDS, counties, reps).transpose(1, 2, 0).reshape(counties, reps * KINDS)
    return jnp.concatenate([age_factor, kind_factor], axis=1)


def spreaders(reps):
    col = jnp.arange(reps * CELLS, dtype=jnp.int32)
    rep_of, cell_of = col // CELLS, col % CELLS
    age_row = jnp.arange(reps * AGES, dtype=jnp.int32)
    kind_row = jnp.arange(reps * KINDS, dtype=jnp.int32)
    to_age = ((age_row[:, None] // AGES == rep_of[None, :])
              & (age_row[:, None] % AGES == cell_of[None, :] // KINDS)).astype(jnp.float32)
    to_kind = ((kind_row[:, None] // KINDS == rep_of[None, :])
               & (kind_row[:, None] % KINDS == cell_of[None, :] % KINDS)).astype(jnp.float32)
    cell_sum = (cell_of[:, None] == jnp.arange(CELLS, dtype=jnp.int32)[None, :]).astype(jnp.float32)
    return to_age, to_kind, cell_sum


def local(weights, cell_ids, group_sizes, group_county, age_rate, kind_rate):
    tables = tabulate(weights, cell_ids, group_sizes)
    groups, width = tables.shape
    reps = width // CELLS
    county = group_county[:, 0]
    owners = lax.axis_size("rows")
    county_here = age_rate.shape[0]
    counties = county_here * owners
    county_range = jnp.arange(counties, dtype=jnp.int32)
    hits = county[None, :] == county_range[:, None]
    partial = exact_dot(hits.astype(jnp.float32), tables)
    present = jnp.sum(hits.astype(jnp.float32), axis=1).reshape(owners, 1, county_here)
    present = jnp.pad(present, ((0, 0), (0, 0), (0, width - county_here)))
    outgoing = jnp.concatenate([partial.reshape(owners, county_here, width), present], axis=1)
    half = width // 2
    core = lax.axis_index("rows") % 2
    low, high = outgoing[:, :, :half], outgoing[:, :, half:]
    keep = jnp.where(core == 0, low, high)
    give = jnp.where(core == 0, high, low)
    keep = keep + lax.ppermute(give, "rows", [(i, i ^ 1) for i in range(owners)])
    arrived = lax.all_to_all(
        keep.reshape(owners * (county_here + 1), half), "rows", 0, 0, tiled=True
    ).reshape(owners // 2, 2, county_here + 1, half)
    summed = jnp.sum(arrived, axis=0)
    county_tables = jnp.concatenate([summed[0, :county_here], summed[1, :county_here]], axis=1)
    groups_in = summed[0, county_here, :county_here]
    factors = rake_own(county_tables, groups_in, age_rate, kind_rate)
    sent = jnp.broadcast_to(factors[None], (owners,) + factors.shape)
    factors = lax.all_to_all(
        sent.reshape(owners * county_here, factors.shape[1]), "rows", 0, 0, tiled=True
    )
    mine = jnp.take(factors, county, axis=0)
    to_age, to_kind, cell_sum = spreaders(reps)
    factor = exact_dot(mine[:, :reps * AGES], to_age) * exact_dot(mine[:, reps * AGES:], to_kind)
    raked = tables * factor

    part_sum = exact_dot(raked, cell_sum)
    part_mean = part_sum / reps
    gap = raked - exact_dot(part_mean, cell_sum.T)
    part_m2 = exact_dot(jnp.square(gap), cell_sum)
    stats = jnp.concatenate([part_sum, part_m2], axis=1)
    shards = lax.axis_size("rep")
    me = lax.axis_index("rep")
    received = [stats] + [
        lax.ppermute(stats, "rep", [(i, (i + s) % shards) for i in range(shards)])
        for s in range(1, shards)
    ]
    by_source = []
    for source in range(shards):
        value = jnp.zeros_like(stats)
        for s in range(shards):
            value = jnp.where((me - s) % shards == source, received[s], value)
        by_source.append(value)
    total_reps = reps * shards
    total = by_source[0][:, :CELLS]
    for source in range(1, shards):
        total = total + by_source[source][:, :CELLS]
    centre = total / total_reps
    deviation = None
    for source in range(shards):
        spread_in = by_source[source][:, CELLS:]
        off_centre = by_source[source][:, :CELLS] / reps - centre
        term = spread_in + reps * jnp.square(off_centre)
        deviation = term if deviation is None else deviation + term
    return (raked, deviation * (4.0 / total_reps))


def solution(mesh):
    placed = (
        P("rep", "rows"),
        P("rows"),
        P("rows", None),
        P("rows", None),
        P("rows", None),
        P("rows", None),
    )
    return jax.shard_map(
        local,
        mesh=mesh,
        in_specs=placed,
        out_specs=(P("rows", "rep"), P("rows", None)),
        check_vma=False,
    )
```

```python
import jax
import jax.numpy as jnp
from jax import lax
from jax.experimental import pallas as pl
from jax.experimental.pallas import tpu as pltpu
from jax.sharding import PartitionSpec as P

AGES = 4
KINDS = 8
CELLS = 32
LOW = 32
ITERS = 4
BLOCK = 128
SPAN = 8
USE_KERNEL = True


def tab_kernel(offs_ref, seg_ref, w_ref, out_ref, acc_ref):
    steps = seg_ref.shape[0]
    width = SPAN * CELLS
    acc_ref[...] = jnp.zeros_like(acc_ref)
    rows = lax.broadcasted_iota(jnp.int32, (width, BLOCK), 0)

    def body(b, carry):
        seg = seg_ref[pl.ds(b, 1), :]
        hot = (rows == seg).astype(jnp.bfloat16)
        start = pl.multiple_of(b * BLOCK, BLOCK)
        w = w_ref[:, pl.ds(start, BLOCK)]
        part = lax.dot_general(
            w, hot, (((1,), (1,)), ((), ())), preferred_element_type=jnp.float32
        )
        off = pl.multiple_of(offs_ref[b], 128)
        acc_ref[:, pl.ds(off, width)] += part
        return carry

    lax.fori_loop(0, steps, body, 0, unroll=8)

    def flip(c, carry):
        block = acc_ref[:, pl.ds(pl.multiple_of(c * width, width), width)]
        out_ref[pl.ds(pl.multiple_of(c * SPAN, SPAN), SPAN), :] = pltpu.einshape(
            "r(gk)->g(rk)", block, g=SPAN, k=CELLS
        )
        return carry

    lax.fori_loop(0, out_ref.shape[0] // SPAN, flip, 0, unroll=4)


def tab_plain(offs, seg, weights, out_width):
    reps = weights.shape[0]
    steps = seg.shape[0]
    width = SPAN * CELLS
    hot = (seg[:, None, :] == jnp.arange(width, dtype=jnp.int32)[None, :, None])
    w = weights.reshape(reps, steps, BLOCK)
    part = jnp.einsum("rbi,bni->brn", w.astype(jnp.float32), hot.astype(jnp.float32),
                      precision=lax.Precision.HIGHEST)
    cols = offs[:, None] + jnp.arange(width, dtype=jnp.int32)[None, :]
    out = jnp.zeros((reps, out_width), jnp.float32)
    return out.at[:, cols.reshape(-1)].add(part.transpose(1, 0, 2).reshape(reps, -1))


def tabulate(weights, cell_ids, group_sizes):
    reps, records = weights.shape
    sizes = group_sizes[0]
    groups = sizes.shape[0]
    ends = jnp.cumsum(sizes).astype(jnp.int32)
    steps = records // BLOCK
    block_start = jnp.arange(steps, dtype=jnp.int32) * BLOCK
    first = jnp.sum((ends[None, :] <= block_start[:, None]).astype(jnp.int32), axis=1)
    base = jnp.minimum(first - first % 4, groups - SPAN).astype(jnp.int32)
    group_range = jnp.arange(groups, dtype=jnp.int32)
    place = block_start[:, None] + jnp.arange(BLOCK, dtype=jnp.int32)[None, :]
    local = jnp.zeros((steps, BLOCK), jnp.int32)
    for j in range(SPAN - 1):
        chosen = group_range[None, :] == (base + j)[:, None]
        edge = jnp.sum(jnp.where(chosen, ends[None, :], 0), axis=1)
        edge = jnp.where(base + j < groups, edge, records + 1)
        local = local + (place >= edge[:, None]).astype(jnp.int32)
    seg = local * CELLS + cell_ids.reshape(steps, BLOCK)
    offs = (base * CELLS).astype(jnp.int32)
    out_width = groups * CELLS
    if USE_KERNEL:
        return pl.pallas_call(
            tab_kernel,
            out_shape=jax.ShapeDtypeStruct((groups, reps * CELLS), jnp.float32),
            in_specs=[
                pl.BlockSpec(memory_space=pltpu.SMEM),
                pl.BlockSpec(memory_space=pltpu.VMEM),
                pl.BlockSpec(memory_space=pltpu.VMEM),
            ],
            out_specs=pl.BlockSpec(memory_space=pltpu.VMEM),
            scratch_shapes=[pltpu.VMEM((reps, out_width), jnp.float32)],
            cost_estimate=pl.CostEstimate(
                flops=2 * reps * records * SPAN * CELLS,
                bytes_accessed=weights.size * 2 + seg.size * 4 + reps * out_width * 4,
                transcendentals=0,
            ),
        )(offs, seg, weights)
    out = tab_plain(offs, seg, weights, out_width).reshape(reps, groups, CELLS)
    return out.transpose(1, 0, 2).reshape(groups, reps * CELLS)


def exact_dot(left, right):
    return jnp.dot(left, right, precision=lax.Precision.HIGHEST, preferred_element_type=jnp.float32)


def rake_own(county_tables, groups_in, age_rate, kind_rate):
    counties, width = county_tables.shape
    reps = width // CELLS
    span = counties * reps
    current = county_tables.reshape(counties, reps, CELLS).transpose(2, 0, 1)
    current = current.reshape(AGES, KINDS, span)
    age_goal = (age_rate * groups_in[:, None]).T
    age_goal = jnp.broadcast_to(age_goal[:, :, None], (AGES, counties, reps)).reshape(AGES, span)
    kind_goal = (kind_rate * groups_in[:, None]).T
    kind_goal = jnp.broadcast_to(kind_goal[:, :, None], (KINDS, counties, reps)).reshape(KINDS, span)
    age_factor = jnp.ones((AGES, span), jnp.float32)
    kind_factor = jnp.ones((KINDS, span), jnp.float32)
    for sweep_index in range(ITERS):
        ratios = age_goal / jnp.maximum(jnp.sum(current, axis=1), 1.0)
        current = current * ratios[:, None, :]
        age_factor = age_factor * ratios
        ratios = kind_goal / jnp.maximum(jnp.sum(current, axis=0), 1.0)
        current = current * ratios[None, :, :]
        kind_factor = kind_factor * ratios
    age_factor = age_factor.reshape(AGES, counties, reps).transpose(1, 2, 0).reshape(counties, reps * AGES)
    kind_factor = kind_factor.reshape(KINDS, counties, reps).transpose(1, 2, 0).reshape(counties, reps * KINDS)
    return jnp.concatenate([age_factor, kind_factor], axis=1)


def spreaders(reps):
    col = jnp.arange(reps * CELLS, dtype=jnp.int32)
    rep_of, cell_of = col // CELLS, col % CELLS
    age_row = jnp.arange(reps * AGES, dtype=jnp.int32)
    kind_row = jnp.arange(reps * KINDS, dtype=jnp.int32)
    to_age = ((age_row[:, None] // AGES == rep_of[None, :])
              & (age_row[:, None] % AGES == cell_of[None, :] // KINDS)).astype(jnp.float32)
    to_kind = ((kind_row[:, None] // KINDS == rep_of[None, :])
               & (kind_row[:, None] % KINDS == cell_of[None, :] % KINDS)).astype(jnp.float32)
    cell_sum = (cell_of[:, None] == jnp.arange(CELLS, dtype=jnp.int32)[None, :]).astype(jnp.float32)
    return to_age, to_kind, cell_sum


def local(weights, cell_ids, group_sizes, group_county, age_rate, kind_rate):
    tables = tabulate(weights, cell_ids, group_sizes)
    groups, width = tables.shape
    reps = width // CELLS
    county = group_county[:, 0]
    owners = lax.axis_size("rows")
    county_here = age_rate.shape[0]
    counties = county_here * owners
    county_range = jnp.arange(counties, dtype=jnp.int32)
    hits = county[None, :] == county_range[:, None]
    partial = exact_dot(hits.astype(jnp.float32), tables)
    present = jnp.sum(hits.astype(jnp.float32), axis=1).reshape(owners, 1, county_here)
    present = jnp.pad(present, ((0, 0), (0, 0), (0, width - county_here)))
    outgoing = jnp.concatenate([partial.reshape(owners, county_here, width), present], axis=1)
    half = width // 2
    core = lax.axis_index("rows") % 2
    low, high = outgoing[:, :, :half], outgoing[:, :, half:]
    keep = jnp.where(core == 0, low, high)
    give = jnp.where(core == 0, high, low)
    keep = keep + lax.ppermute(give, "rows", [(i, i ^ 1) for i in range(owners)])
    arrived = lax.all_to_all(
        keep.reshape(owners * (county_here + 1), half), "rows", 0, 0, tiled=True
    ).reshape(owners // 2, 2, county_here + 1, half)
    summed = jnp.sum(arrived, axis=0)
    county_tables = jnp.concatenate([summed[0, :county_here], summed[1, :county_here]], axis=1)
    groups_in = summed[0, county_here, :county_here]
    factors = rake_own(county_tables, groups_in, age_rate, kind_rate)
    sent = jnp.broadcast_to(factors[None], (owners,) + factors.shape)
    factors = lax.all_to_all(
        sent.reshape(owners * county_here, factors.shape[1]), "rows", 0, 0, tiled=True
    )
    mine = jnp.take(factors, county, axis=0)
    to_age, to_kind, cell_sum = spreaders(reps)
    factor = exact_dot(mine[:, :reps * AGES], to_age) * exact_dot(mine[:, reps * AGES:], to_kind)
    raked = tables * factor

    part_sum = exact_dot(raked, cell_sum)
    part_mean = part_sum / reps
    gap = raked - exact_dot(part_mean, cell_sum.T)
    part_m2 = exact_dot(jnp.square(gap), cell_sum)
    stats = jnp.concatenate([part_sum, part_m2], axis=1)
    shards = lax.axis_size("rep")
    me = lax.axis_index("rep")
    received = [stats] + [
        lax.ppermute(stats, "rep", [(i, (i + s) % shards) for i in range(shards)])
        for s in range(1, shards)
    ]
    by_source = []
    for source in range(shards):
        value = jnp.zeros_like(stats)
        for s in range(shards):
            value = jnp.where((me - s) % shards == source, received[s], value)
        by_source.append(value)
    total_reps = reps * shards
    total = by_source[0][:, :CELLS]
    for source in range(1, shards):
        total = total + by_source[source][:, :CELLS]
    centre = total / total_reps
    deviation = None
    for source in range(shards):
        spread_in = by_source[source][:, CELLS:]
        off_centre = by_source[source][:, :CELLS] / reps - centre
        term = spread_in + reps * jnp.square(off_centre)
        deviation = term if deviation is None else deviation + term
    return (raked, deviation * (4.0 / total_reps))


def solution(mesh):
    placed = (
        P("rep", "rows"),
        P("rows"),
        P("rows", None),
        P("rows", None),
        P("rows", None),
        P("rows", None),
    )
    return jax.shard_map(
        local,
        mesh=mesh,
        in_specs=placed,
        out_specs=(P("rows", "rep"), P("rows", None)),
        check_vma=False,
    )
```

```python
import jax
import jax.numpy as jnp
from jax import lax
from jax.experimental import pallas as pl
from jax.experimental.pallas import tpu as pltpu
from jax.sharding import PartitionSpec as P

AGES = 4
KINDS = 8
CELLS = 32
LOW = 32
ITERS = 4
BLOCK = 256
SPAN = 12
USE_KERNEL = True


def tab_kernel(offs_ref, seg_ref, w_ref, out_ref):
    steps = seg_ref.shape[0]
    width = SPAN * CELLS
    out_ref[...] = jnp.zeros_like(out_ref)
    rows = lax.broadcasted_iota(jnp.int32, (width, BLOCK), 0)

    def body(b, carry):
        seg = seg_ref[pl.ds(b, 1), :]
        hot = (rows == seg).astype(jnp.bfloat16)
        start = pl.multiple_of(b * BLOCK, BLOCK)
        w = w_ref[:, pl.ds(start, BLOCK)]
        part = lax.dot_general(
            w, hot, (((1,), (1,)), ((), ())), preferred_element_type=jnp.float32
        )
        off = pl.multiple_of(offs_ref[b], 128)
        out_ref[:, pl.ds(off, width)] += part
        return carry

    lax.fori_loop(0, steps, body, 0, unroll=8)


def tab_plain(offs, seg, weights, out_width):
    reps = weights.shape[0]
    steps = seg.shape[0]
    width = SPAN * CELLS
    hot = (seg[:, None, :] == jnp.arange(width, dtype=jnp.int32)[None, :, None])
    w = weights.reshape(reps, steps, BLOCK)
    part = jnp.einsum("rbi,bni->brn", w.astype(jnp.float32), hot.astype(jnp.float32),
                      precision=lax.Precision.HIGHEST)
    cols = offs[:, None] + jnp.arange(width, dtype=jnp.int32)[None, :]
    out = jnp.zeros((reps, out_width), jnp.float32)
    return out.at[:, cols.reshape(-1)].add(part.transpose(1, 0, 2).reshape(reps, -1))


def tabulate(weights, cell_ids, group_sizes):
    reps, records = weights.shape
    sizes = group_sizes[0]
    groups = sizes.shape[0]
    ends = jnp.cumsum(sizes).astype(jnp.int32)
    steps = records // BLOCK
    block_start = jnp.arange(steps, dtype=jnp.int32) * BLOCK
    first = jnp.sum((ends[None, :] <= block_start[:, None]).astype(jnp.int32), axis=1)
    base = jnp.minimum(first - first % 4, groups - SPAN).astype(jnp.int32)
    group_range = jnp.arange(groups, dtype=jnp.int32)
    place = block_start[:, None] + jnp.arange(BLOCK, dtype=jnp.int32)[None, :]
    local = jnp.zeros((steps, BLOCK), jnp.int32)
    for j in range(SPAN - 1):
        chosen = group_range[None, :] == (base + j)[:, None]
        edge = jnp.sum(jnp.where(chosen, ends[None, :], 0), axis=1)
        edge = jnp.where(base + j < groups, edge, records + 1)
        local = local + (place >= edge[:, None]).astype(jnp.int32)
    seg = local * CELLS + cell_ids.reshape(steps, BLOCK)
    offs = (base * CELLS).astype(jnp.int32)
    out_width = groups * CELLS
    if USE_KERNEL:
        out = pl.pallas_call(
            tab_kernel,
            out_shape=jax.ShapeDtypeStruct((reps, out_width), jnp.float32),
            in_specs=[
                pl.BlockSpec(memory_space=pltpu.SMEM),
                pl.BlockSpec(memory_space=pltpu.VMEM),
                pl.BlockSpec(memory_space=pltpu.VMEM),
            ],
            out_specs=pl.BlockSpec(memory_space=pltpu.VMEM),
            cost_estimate=pl.CostEstimate(
                flops=2 * reps * records * SPAN * CELLS,
                bytes_accessed=weights.size * 2 + seg.size * 4 + reps * out_width * 4,
                transcendentals=0,
            ),
        )(offs, seg, weights)
    else:
        out = tab_plain(offs, seg, weights, out_width)
    out = out.reshape(reps, groups, CELLS)
    return out.transpose(1, 0, 2).reshape(groups, reps * CELLS)


def exact_dot(left, right):
    return jnp.dot(left, right, precision=lax.Precision.HIGHEST, preferred_element_type=jnp.float32)


def rake_own(county_tables, groups_in, age_rate, kind_rate):
    counties, width = county_tables.shape
    reps = width // CELLS
    span = counties * reps
    current = county_tables.reshape(counties, reps, CELLS).transpose(2, 0, 1)
    current = current.reshape(AGES, KINDS, span)
    age_goal = (age_rate * groups_in[:, None]).T
    age_goal = jnp.broadcast_to(age_goal[:, :, None], (AGES, counties, reps)).reshape(AGES, span)
    kind_goal = (kind_rate * groups_in[:, None]).T
    kind_goal = jnp.broadcast_to(kind_goal[:, :, None], (KINDS, counties, reps)).reshape(KINDS, span)
    age_factor = jnp.ones((AGES, span), jnp.float32)
    kind_factor = jnp.ones((KINDS, span), jnp.float32)
    for sweep_index in range(ITERS):
        ratios = age_goal / jnp.maximum(jnp.sum(current, axis=1), 1.0)
        current = current * ratios[:, None, :]
        age_factor = age_factor * ratios
        ratios = kind_goal / jnp.maximum(jnp.sum(current, axis=0), 1.0)
        current = current * ratios[None, :, :]
        kind_factor = kind_factor * ratios
    age_factor = age_factor.reshape(AGES, counties, reps).transpose(1, 2, 0).reshape(counties, reps * AGES)
    kind_factor = kind_factor.reshape(KINDS, counties, reps).transpose(1, 2, 0).reshape(counties, reps * KINDS)
    return jnp.concatenate([age_factor, kind_factor], axis=1)


def spreaders(reps):
    col = jnp.arange(reps * CELLS, dtype=jnp.int32)
    rep_of, cell_of = col // CELLS, col % CELLS
    age_row = jnp.arange(reps * AGES, dtype=jnp.int32)
    kind_row = jnp.arange(reps * KINDS, dtype=jnp.int32)
    to_age = ((age_row[:, None] // AGES == rep_of[None, :])
              & (age_row[:, None] % AGES == cell_of[None, :] // KINDS)).astype(jnp.float32)
    to_kind = ((kind_row[:, None] // KINDS == rep_of[None, :])
               & (kind_row[:, None] % KINDS == cell_of[None, :] % KINDS)).astype(jnp.float32)
    cell_sum = (cell_of[:, None] == jnp.arange(CELLS, dtype=jnp.int32)[None, :]).astype(jnp.float32)
    return to_age, to_kind, cell_sum


def local(weights, cell_ids, group_sizes, group_county, age_rate, kind_rate):
    tables = tabulate(weights, cell_ids, group_sizes)
    groups, width = tables.shape
    reps = width // CELLS
    county = group_county[:, 0]
    owners = lax.axis_size("rows")
    county_here = age_rate.shape[0]
    counties = county_here * owners
    county_range = jnp.arange(counties, dtype=jnp.int32)
    hits = county[None, :] == county_range[:, None]
    partial = exact_dot(hits.astype(jnp.float32), tables)
    present = jnp.sum(hits.astype(jnp.float32), axis=1).reshape(owners, 1, county_here)
    present = jnp.pad(present, ((0, 0), (0, 0), (0, width - county_here)))
    outgoing = jnp.concatenate([partial.reshape(owners, county_here, width), present], axis=1)
    half = width // 2
    core = lax.axis_index("rows") % 2
    low, high = outgoing[:, :, :half], outgoing[:, :, half:]
    keep = jnp.where(core == 0, low, high)
    give = jnp.where(core == 0, high, low)
    keep = keep + lax.ppermute(give, "rows", [(i, i ^ 1) for i in range(owners)])
    arrived = lax.all_to_all(
        keep.reshape(owners * (county_here + 1), half), "rows", 0, 0, tiled=True
    ).reshape(owners // 2, 2, county_here + 1, half)
    summed = jnp.sum(arrived, axis=0)
    county_tables = jnp.concatenate([summed[0, :county_here], summed[1, :county_here]], axis=1)
    groups_in = summed[0, county_here, :county_here]
    factors = rake_own(county_tables, groups_in, age_rate, kind_rate)
    sent = jnp.broadcast_to(factors[None], (owners,) + factors.shape)
    factors = lax.all_to_all(
        sent.reshape(owners * county_here, factors.shape[1]), "rows", 0, 0, tiled=True
    )
    mine = jnp.take(factors, county, axis=0)
    to_age, to_kind, cell_sum = spreaders(reps)
    factor = exact_dot(mine[:, :reps * AGES], to_age) * exact_dot(mine[:, reps * AGES:], to_kind)
    raked = tables * factor

    part_sum = exact_dot(raked, cell_sum)
    part_mean = part_sum / reps
    gap = raked - exact_dot(part_mean, cell_sum.T)
    part_m2 = exact_dot(jnp.square(gap), cell_sum)
    stats = jnp.concatenate([part_sum, part_m2], axis=1)
    shards = lax.axis_size("rep")
    sent = jnp.broadcast_to(stats[None], (shards,) + stats.shape)
    received = lax.all_to_all(
        sent.reshape(shards * groups, stats.shape[1]), "rep", 0, 0, tiled=True
    ).reshape(shards, groups, stats.shape[1])
    by_source = [received[source] for source in range(shards)]
    total_reps = reps * shards
    total = by_source[0][:, :CELLS]
    for source in range(1, shards):
        total = total + by_source[source][:, :CELLS]
    centre = total / total_reps
    deviation = None
    for source in range(shards):
        spread_in = by_source[source][:, CELLS:]
        off_centre = by_source[source][:, :CELLS] / reps - centre
        term = spread_in + reps * jnp.square(off_centre)
        deviation = term if deviation is None else deviation + term
    return (raked, deviation * (4.0 / total_reps))


def solution(mesh):
    placed = (
        P("rep", "rows"),
        P("rows"),
        P("rows", None),
        P("rows", None),
        P("rows", None),
        P("rows", None),
    )
    return jax.shard_map(
        local,
        mesh=mesh,
        in_specs=placed,
        out_specs=(P("rows", "rep"), P("rows", None)),
        check_vma=False,
    )
```

```python
import jax
import jax.numpy as jnp
from jax import lax
from jax.experimental import pallas as pl
from jax.experimental.pallas import tpu as pltpu
from jax.sharding import PartitionSpec as P

AGES = 4
KINDS = 8
CELLS = 32
LOW = 32
ITERS = 4
BLOCK = 256
SPAN = 12
USE_KERNEL = True


def tab_kernel(offs_ref, seg_ref, w_ref, out_ref):
    steps = seg_ref.shape[0]
    width = SPAN * CELLS
    out_ref[...] = jnp.zeros_like(out_ref)
    rows = lax.broadcasted_iota(jnp.int32, (width, BLOCK), 0)

    def body(b, carry):
        seg = seg_ref[pl.ds(b, 1), :]
        hot = (rows == seg).astype(jnp.bfloat16)
        start = pl.multiple_of(b * BLOCK, BLOCK)
        w = w_ref[:, pl.ds(start, BLOCK)]
        part = lax.dot_general(
            w, hot, (((1,), (1,)), ((), ())), preferred_element_type=jnp.float32
        )
        off = pl.multiple_of(offs_ref[b], 128)
        out_ref[:, pl.ds(off, width)] += part
        return carry

    lax.fori_loop(0, steps, body, 0, unroll=8)


def tab_plain(offs, seg, weights, out_width):
    reps = weights.shape[0]
    steps = seg.shape[0]
    width = SPAN * CELLS
    hot = (seg[:, None, :] == jnp.arange(width, dtype=jnp.int32)[None, :, None])
    w = weights.reshape(reps, steps, BLOCK)
    part = jnp.einsum("rbi,bni->brn", w.astype(jnp.float32), hot.astype(jnp.float32),
                      precision=lax.Precision.HIGHEST)
    cols = offs[:, None] + jnp.arange(width, dtype=jnp.int32)[None, :]
    out = jnp.zeros((reps, out_width), jnp.float32)
    return out.at[:, cols.reshape(-1)].add(part.transpose(1, 0, 2).reshape(reps, -1))


def tabulate(weights, cell_ids, group_sizes):
    reps, records = weights.shape
    sizes = group_sizes[0]
    groups = sizes.shape[0]
    ends = jnp.cumsum(sizes).astype(jnp.int32)
    steps = records // BLOCK
    block_start = jnp.arange(steps, dtype=jnp.int32) * BLOCK
    first = jnp.sum((ends[None, :] <= block_start[:, None]).astype(jnp.int32), axis=1)
    base = jnp.minimum(first - first % 4, groups - SPAN).astype(jnp.int32)
    group_range = jnp.arange(groups, dtype=jnp.int32)
    place = block_start[:, None] + jnp.arange(BLOCK, dtype=jnp.int32)[None, :]
    local = jnp.zeros((steps, BLOCK), jnp.int32)
    for j in range(SPAN - 1):
        chosen = group_range[None, :] == (base + j)[:, None]
        edge = jnp.sum(jnp.where(chosen, ends[None, :], 0), axis=1)
        edge = jnp.where(base + j < groups, edge, records + 1)
        local = local + (place >= edge[:, None]).astype(jnp.int32)
    seg = local * CELLS + cell_ids.reshape(steps, BLOCK)
    offs = (base * CELLS).astype(jnp.int32)
    out_width = groups * CELLS
    if USE_KERNEL:
        out = pl.pallas_call(
            tab_kernel,
            out_shape=jax.ShapeDtypeStruct((reps, out_width), jnp.float32),
            in_specs=[
                pl.BlockSpec(memory_space=pltpu.SMEM),
                pl.BlockSpec(memory_space=pltpu.VMEM),
                pl.BlockSpec(memory_space=pltpu.VMEM),
            ],
            out_specs=pl.BlockSpec(memory_space=pltpu.VMEM),
            cost_estimate=pl.CostEstimate(
                flops=2 * reps * records * SPAN * CELLS,
                bytes_accessed=weights.size * 2 + seg.size * 4 + reps * out_width * 4,
                transcendentals=0,
            ),
        )(offs, seg, weights)
    else:
        out = tab_plain(offs, seg, weights, out_width)
    out = out.reshape(reps, groups, CELLS)
    return out.transpose(1, 0, 2).reshape(groups, reps * CELLS)


def exact_dot(left, right):
    return jnp.dot(left, right, precision=lax.Precision.HIGHEST, preferred_element_type=jnp.float32)


def rake_own(county_tables, groups_in, age_rate, kind_rate):
    counties, width = county_tables.shape
    reps = width // CELLS
    span = counties * reps
    current = county_tables.reshape(counties, reps, CELLS).transpose(2, 0, 1)
    current = current.reshape(AGES, KINDS, span)
    age_goal = (age_rate * groups_in[:, None]).T
    age_goal = jnp.broadcast_to(age_goal[:, :, None], (AGES, counties, reps)).reshape(AGES, span)
    kind_goal = (kind_rate * groups_in[:, None]).T
    kind_goal = jnp.broadcast_to(kind_goal[:, :, None], (KINDS, counties, reps)).reshape(KINDS, span)
    age_factor = jnp.ones((AGES, span), jnp.float32)
    kind_factor = jnp.ones((KINDS, span), jnp.float32)
    for sweep_index in range(ITERS):
        ratios = age_goal / jnp.maximum(jnp.sum(current, axis=1), 1.0)
        current = current * ratios[:, None, :]
        age_factor = age_factor * ratios
        ratios = kind_goal / jnp.maximum(jnp.sum(current, axis=0), 1.0)
        current = current * ratios[None, :, :]
        kind_factor = kind_factor * ratios
    age_factor = age_factor.reshape(AGES, counties, reps).transpose(1, 2, 0).reshape(counties, reps * AGES)
    kind_factor = kind_factor.reshape(KINDS, counties, reps).transpose(1, 2, 0).reshape(counties, reps * KINDS)
    return jnp.concatenate([age_factor, kind_factor], axis=1)


def spreaders(reps):
    col = jnp.arange(reps * CELLS, dtype=jnp.int32)
    rep_of, cell_of = col // CELLS, col % CELLS
    age_row = jnp.arange(reps * AGES, dtype=jnp.int32)
    kind_row = jnp.arange(reps * KINDS, dtype=jnp.int32)
    to_age = ((age_row[:, None] // AGES == rep_of[None, :])
              & (age_row[:, None] % AGES == cell_of[None, :] // KINDS)).astype(jnp.float32)
    to_kind = ((kind_row[:, None] // KINDS == rep_of[None, :])
               & (kind_row[:, None] % KINDS == cell_of[None, :] % KINDS)).astype(jnp.float32)
    cell_sum = (cell_of[:, None] == jnp.arange(CELLS, dtype=jnp.int32)[None, :]).astype(jnp.float32)
    return to_age, to_kind, cell_sum


def local(weights, cell_ids, group_sizes, group_county, age_rate, kind_rate):
    tables = tabulate(weights, cell_ids, group_sizes)
    groups, width = tables.shape
    reps = width // CELLS
    county = group_county[:, 0]
    owners = lax.axis_size("rows")
    county_here = age_rate.shape[0]
    counties = county_here * owners
    county_range = jnp.arange(counties, dtype=jnp.int32)
    hits = county[None, :] == county_range[:, None]
    partial = exact_dot(hits.astype(jnp.float32), tables)
    present = jnp.sum(hits.astype(jnp.float32), axis=1).reshape(owners, 1, county_here)
    present = jnp.pad(present, ((0, 0), (0, 0), (0, width - county_here)))
    outgoing = jnp.concatenate([partial.reshape(owners, county_here, width), present], axis=1)
    half = width // 2
    core = lax.axis_index("rows") % 2
    low, high = outgoing[:, :, :half], outgoing[:, :, half:]
    keep = jnp.where(core == 0, low, high)
    give = jnp.where(core == 0, high, low)
    keep = keep + lax.ppermute(give, "rows", [(i, i ^ 1) for i in range(owners)])
    me = lax.axis_index("rows")
    rolled = lax.dynamic_slice_in_dim(jnp.concatenate([keep, keep], axis=0), me, owners, 0)
    same_half = rolled[0]
    other_half = jnp.zeros_like(same_half)
    for shift in range(1, owners):
        block = rolled[shift]
        got = lax.ppermute(block, "rows", [(i, (i + shift) % owners) for i in range(owners)])
        if shift % 2:
            other_half = other_half + got
        else:
            same_half = same_half + got
    low = jnp.where(core == 0, same_half, other_half)
    high = jnp.where(core == 0, other_half, same_half)
    county_tables = jnp.concatenate([low[:county_here], high[:county_here]], axis=1)
    groups_in = low[county_here, :county_here]
    factors = rake_own(county_tables, groups_in, age_rate, kind_rate)
    sent = jnp.broadcast_to(factors[None], (owners,) + factors.shape)
    factors = lax.all_to_all(
        sent.reshape(owners * county_here, factors.shape[1]), "rows", 0, 0, tiled=True
    )
    mine = jnp.take(factors, county, axis=0)
    to_age, to_kind, cell_sum = spreaders(reps)
    factor = exact_dot(mine[:, :reps * AGES], to_age) * exact_dot(mine[:, reps * AGES:], to_kind)
    raked = tables * factor

    part_sum = exact_dot(raked, cell_sum)
    part_mean = part_sum / reps
    gap = raked - exact_dot(part_mean, cell_sum.T)
    part_m2 = exact_dot(jnp.square(gap), cell_sum)
    stats = jnp.concatenate([part_sum, part_m2], axis=1)
    shards = lax.axis_size("rep")
    sent = jnp.broadcast_to(stats[None], (shards,) + stats.shape)
    received = lax.all_to_all(
        sent.reshape(shards * groups, stats.shape[1]), "rep", 0, 0, tiled=True
    ).reshape(shards, groups, stats.shape[1])
    by_source = [received[source] for source in range(shards)]
    total_reps = reps * shards
    total = by_source[0][:, :CELLS]
    for source in range(1, shards):
        total = total + by_source[source][:, :CELLS]
    centre = total / total_reps
    deviation = None
    for source in range(shards):
        spread_in = by_source[source][:, CELLS:]
        off_centre = by_source[source][:, :CELLS] / reps - centre
        term = spread_in + reps * jnp.square(off_centre)
        deviation = term if deviation is None else deviation + term
    return (raked, deviation * (4.0 / total_reps))


def solution(mesh):
    placed = (
        P("rep", "rows"),
        P("rows"),
        P("rows", None),
        P("rows", None),
        P("rows", None),
        P("rows", None),
    )
    return jax.shard_map(
        local,
        mesh=mesh,
        in_specs=placed,
        out_specs=(P("rows", "rep"), P("rows", None)),
        check_vma=False,
    )
```

```python
import jax
import jax.numpy as jnp
from jax import lax
from jax.experimental import pallas as pl
from jax.experimental.pallas import tpu as pltpu
from jax.sharding import PartitionSpec as P

AGES = 4
KINDS = 8
CELLS = 32
LOW = 32
ITERS = 4
BLOCK = 256
SPAN = 12
USE_KERNEL = True


def tab_kernel(offs_ref, seg_ref, w_ref, out_ref):
    steps = seg_ref.shape[0]
    width = SPAN * CELLS
    out_ref[...] = jnp.zeros_like(out_ref)
    rows = lax.broadcasted_iota(jnp.int32, (width, BLOCK), 0)

    def body(b, carry):
        seg = seg_ref[pl.ds(b, 1), :]
        hot = (rows == seg).astype(jnp.bfloat16)
        start = pl.multiple_of(b * BLOCK, BLOCK)
        w = w_ref[:, pl.ds(start, BLOCK)]
        part = lax.dot_general(
            w, hot, (((1,), (1,)), ((), ())), preferred_element_type=jnp.float32
        )
        off = pl.multiple_of(offs_ref[b], 128)
        out_ref[:, pl.ds(off, width)] += part
        return carry

    lax.fori_loop(0, steps, body, 0, unroll=16)


def tab_plain(offs, seg, weights, out_width):
    reps = weights.shape[0]
    steps = seg.shape[0]
    width = SPAN * CELLS
    hot = (seg[:, None, :] == jnp.arange(width, dtype=jnp.int32)[None, :, None])
    w = weights.reshape(reps, steps, BLOCK)
    part = jnp.einsum("rbi,bni->brn", w.astype(jnp.float32), hot.astype(jnp.float32),
                      precision=lax.Precision.HIGHEST)
    cols = offs[:, None] + jnp.arange(width, dtype=jnp.int32)[None, :]
    out = jnp.zeros((reps, out_width), jnp.float32)
    return out.at[:, cols.reshape(-1)].add(part.transpose(1, 0, 2).reshape(reps, -1))


def tabulate(weights, cell_ids, group_sizes):
    reps, records = weights.shape
    sizes = group_sizes[0]
    groups = sizes.shape[0]
    ends = jnp.cumsum(sizes).astype(jnp.int32)
    steps = records // BLOCK
    block_start = jnp.arange(steps, dtype=jnp.int32) * BLOCK
    first = jnp.sum((ends[None, :] <= block_start[:, None]).astype(jnp.int32), axis=1)
    base = jnp.minimum(first - first % 4, groups - SPAN).astype(jnp.int32)
    group_range = jnp.arange(groups, dtype=jnp.int32)
    place = block_start[:, None] + jnp.arange(BLOCK, dtype=jnp.int32)[None, :]
    local = jnp.zeros((steps, BLOCK), jnp.int32)
    for j in range(SPAN - 1):
        chosen = group_range[None, :] == (base + j)[:, None]
        edge = jnp.sum(jnp.where(chosen, ends[None, :], 0), axis=1)
        edge = jnp.where(base + j < groups, edge, records + 1)
        local = local + (place >= edge[:, None]).astype(jnp.int32)
    seg = local * CELLS + cell_ids.reshape(steps, BLOCK)
    offs = (base * CELLS).astype(jnp.int32)
    out_width = groups * CELLS
    if USE_KERNEL:
        out = pl.pallas_call(
            tab_kernel,
            out_shape=jax.ShapeDtypeStruct((reps, out_width), jnp.float32),
            in_specs=[
                pl.BlockSpec(memory_space=pltpu.SMEM),
                pl.BlockSpec(memory_space=pltpu.VMEM),
                pl.BlockSpec(memory_space=pltpu.VMEM),
            ],
            out_specs=pl.BlockSpec(memory_space=pltpu.VMEM),
            cost_estimate=pl.CostEstimate(
                flops=2 * reps * records * SPAN * CELLS,
                bytes_accessed=weights.size * 2 + seg.size * 4 + reps * out_width * 4,
                transcendentals=0,
            ),
        )(offs, seg, weights)
    else:
        out = tab_plain(offs, seg, weights, out_width)
    out = out.reshape(reps, groups, CELLS)
    return out.transpose(1, 0, 2).reshape(groups, reps * CELLS)


def exact_dot(left, right):
    return jnp.dot(left, right, precision=lax.Precision.HIGHEST, preferred_element_type=jnp.float32)


def rake_own(county_tables, groups_in, age_rate, kind_rate):
    counties, width = county_tables.shape
    reps = width // CELLS
    span = counties * reps
    current = county_tables.reshape(counties, reps, CELLS).transpose(2, 0, 1)
    current = current.reshape(AGES, KINDS, span)
    age_goal = (age_rate * groups_in[:, None]).T
    age_goal = jnp.broadcast_to(age_goal[:, :, None], (AGES, counties, reps)).reshape(AGES, span)
    kind_goal = (kind_rate * groups_in[:, None]).T
    kind_goal = jnp.broadcast_to(kind_goal[:, :, None], (KINDS, counties, reps)).reshape(KINDS, span)
    age_factor = jnp.ones((AGES, span), jnp.float32)
    kind_factor = jnp.ones((KINDS, span), jnp.float32)
    for sweep_index in range(ITERS):
        ratios = age_goal / jnp.maximum(jnp.sum(current, axis=1), 1.0)
        current = current * ratios[:, None, :]
        age_factor = age_factor * ratios
        ratios = kind_goal / jnp.maximum(jnp.sum(current, axis=0), 1.0)
        current = current * ratios[None, :, :]
        kind_factor = kind_factor * ratios
    age_factor = age_factor.reshape(AGES, counties, reps).transpose(1, 2, 0).reshape(counties, reps * AGES)
    kind_factor = kind_factor.reshape(KINDS, counties, reps).transpose(1, 2, 0).reshape(counties, reps * KINDS)
    return jnp.concatenate([age_factor, kind_factor], axis=1)


def spreaders(reps):
    col = jnp.arange(reps * CELLS, dtype=jnp.int32)
    rep_of, cell_of = col // CELLS, col % CELLS
    age_row = jnp.arange(reps * AGES, dtype=jnp.int32)
    kind_row = jnp.arange(reps * KINDS, dtype=jnp.int32)
    to_age = ((age_row[:, None] // AGES == rep_of[None, :])
              & (age_row[:, None] % AGES == cell_of[None, :] // KINDS)).astype(jnp.float32)
    to_kind = ((kind_row[:, None] // KINDS == rep_of[None, :])
               & (kind_row[:, None] % KINDS == cell_of[None, :] % KINDS)).astype(jnp.float32)
    cell_sum = (cell_of[:, None] == jnp.arange(CELLS, dtype=jnp.int32)[None, :]).astype(jnp.float32)
    return to_age, to_kind, cell_sum


def local(weights, cell_ids, group_sizes, group_county, age_rate, kind_rate):
    tables = tabulate(weights, cell_ids, group_sizes)
    groups, width = tables.shape
    reps = width // CELLS
    county = group_county[:, 0]
    owners = lax.axis_size("rows")
    county_here = age_rate.shape[0]
    counties = county_here * owners
    county_range = jnp.arange(counties, dtype=jnp.int32)
    hits = county[None, :] == county_range[:, None]
    partial = exact_dot(hits.astype(jnp.float32), tables)
    present = jnp.sum(hits.astype(jnp.float32), axis=1).reshape(owners, 1, county_here)
    present = jnp.pad(present, ((0, 0), (0, 0), (0, width - county_here)))
    outgoing = jnp.concatenate([partial.reshape(owners, county_here, width), present], axis=1)
    half = width // 2
    core = lax.axis_index("rows") % 2
    low, high = outgoing[:, :, :half], outgoing[:, :, half:]
    keep = jnp.where(core == 0, low, high)
    give = jnp.where(core == 0, high, low)
    keep = keep + lax.ppermute(give, "rows", [(i, i ^ 1) for i in range(owners)])
    arrived = lax.all_to_all(
        keep.reshape(owners * (county_here + 1), half), "rows", 0, 0, tiled=True
    ).reshape(owners // 2, 2, county_here + 1, half)
    summed = jnp.sum(arrived, axis=0)
    county_tables = jnp.concatenate([summed[0, :county_here], summed[1, :county_here]], axis=1)
    groups_in = summed[0, county_here, :county_here]
    factors = rake_own(county_tables, groups_in, age_rate, kind_rate)
    sent = jnp.broadcast_to(factors[None], (owners,) + factors.shape)
    factors = lax.all_to_all(
        sent.reshape(owners * county_here, factors.shape[1]), "rows", 0, 0, tiled=True
    )
    mine = jnp.take(factors, county, axis=0)
    to_age, to_kind, cell_sum = spreaders(reps)
    factor = exact_dot(mine[:, :reps * AGES], to_age) * exact_dot(mine[:, reps * AGES:], to_kind)
    raked = tables * factor

    part_sum = exact_dot(raked, cell_sum)
    part_mean = part_sum / reps
    gap = raked - exact_dot(part_mean, cell_sum.T)
    part_m2 = exact_dot(jnp.square(gap), cell_sum)
    stats = jnp.concatenate([part_sum, part_m2], axis=1)
    shards = lax.axis_size("rep")
    sent = jnp.broadcast_to(stats[None], (shards,) + stats.shape)
    received = lax.all_to_all(
        sent.reshape(shards * groups, stats.shape[1]), "rep", 0, 0, tiled=True
    ).reshape(shards, groups, stats.shape[1])
    by_source = [received[source] for source in range(shards)]
    total_reps = reps * shards
    total = by_source[0][:, :CELLS]
    for source in range(1, shards):
        total = total + by_source[source][:, :CELLS]
    centre = total / total_reps
    deviation = None
    for source in range(shards):
        spread_in = by_source[source][:, CELLS:]
        off_centre = by_source[source][:, :CELLS] / reps - centre
        term = spread_in + reps * jnp.square(off_centre)
        deviation = term if deviation is None else deviation + term
    return (raked, deviation * (4.0 / total_reps))


def solution(mesh):
    placed = (
        P("rep", "rows"),
        P("rows"),
        P("rows", None),
        P("rows", None),
        P("rows", None),
        P("rows", None),
    )
    return jax.shard_map(
        local,
        mesh=mesh,
        in_specs=placed,
        out_specs=(P("rows", "rep"), P("rows", None)),
        check_vma=False,
    )
```

```python
import jax
import jax.numpy as jnp
from jax import lax
from jax.experimental import pallas as pl
from jax.experimental.pallas import tpu as pltpu
from jax.sharding import PartitionSpec as P

AGES = 4
KINDS = 8
CELLS = 32
LOW = 32
ITERS = 4
BLOCK = 256
SPAN = 12
USE_KERNEL = True


def tab_kernel(offs_ref, seg_ref, w_ref, out_ref):
    steps = seg_ref.shape[0]
    width = SPAN * CELLS
    out_ref[...] = jnp.zeros_like(out_ref)
    rows = lax.broadcasted_iota(jnp.int32, (width, BLOCK), 0)

    def body(b, carry):
        seg = seg_ref[pl.ds(b, 1), :]
        hot = (rows == seg).astype(jnp.bfloat16)
        start = pl.multiple_of(b * BLOCK, BLOCK)
        w = w_ref[:, pl.ds(start, BLOCK)]
        part = lax.dot_general(
            w, hot, (((1,), (1,)), ((), ())), preferred_element_type=jnp.float32
        )
        off = pl.multiple_of(offs_ref[b], 128)
        out_ref[:, pl.ds(off, width)] += part
        return carry

    lax.fori_loop(0, steps, body, 0, unroll=32)


def tab_plain(offs, seg, weights, out_width):
    reps = weights.shape[0]
    steps = seg.shape[0]
    width = SPAN * CELLS
    hot = (seg[:, None, :] == jnp.arange(width, dtype=jnp.int32)[None, :, None])
    w = weights.reshape(reps, steps, BLOCK)
    part = jnp.einsum("rbi,bni->brn", w.astype(jnp.float32), hot.astype(jnp.float32),
                      precision=lax.Precision.HIGHEST)
    cols = offs[:, None] + jnp.arange(width, dtype=jnp.int32)[None, :]
    out = jnp.zeros((reps, out_width), jnp.float32)
    return out.at[:, cols.reshape(-1)].add(part.transpose(1, 0, 2).reshape(reps, -1))


def tabulate(weights, cell_ids, group_sizes):
    reps, records = weights.shape
    sizes = group_sizes[0]
    groups = sizes.shape[0]
    ends = jnp.cumsum(sizes).astype(jnp.int32)
    steps = records // BLOCK
    block_start = jnp.arange(steps, dtype=jnp.int32) * BLOCK
    first = jnp.sum((ends[None, :] <= block_start[:, None]).astype(jnp.int32), axis=1)
    base = jnp.minimum(first - first % 4, groups - SPAN).astype(jnp.int32)
    group_range = jnp.arange(groups, dtype=jnp.int32)
    place = block_start[:, None] + jnp.arange(BLOCK, dtype=jnp.int32)[None, :]
    local = jnp.zeros((steps, BLOCK), jnp.int32)
    for j in range(SPAN - 1):
        chosen = group_range[None, :] == (base + j)[:, None]
        edge = jnp.sum(jnp.where(chosen, ends[None, :], 0), axis=1)
        edge = jnp.where(base + j < groups, edge, records + 1)
        local = local + (place >= edge[:, None]).astype(jnp.int32)
    seg = local * CELLS + cell_ids.reshape(steps, BLOCK)
    offs = (base * CELLS).astype(jnp.int32)
    out_width = groups * CELLS
    if USE_KERNEL:
        out = pl.pallas_call(
            tab_kernel,
            out_shape=jax.ShapeDtypeStruct((reps, out_width), jnp.float32),
            in_specs=[
                pl.BlockSpec(memory_space=pltpu.SMEM),
                pl.BlockSpec(memory_space=pltpu.VMEM),
                pl.BlockSpec(memory_space=pltpu.VMEM),
            ],
            out_specs=pl.BlockSpec(memory_space=pltpu.VMEM),
            cost_estimate=pl.CostEstimate(
                flops=2 * reps * records * SPAN * CELLS,
                bytes_accessed=weights.size * 2 + seg.size * 4 + reps * out_width * 4,
                transcendentals=0,
            ),
        )(offs, seg, weights)
    else:
        out = tab_plain(offs, seg, weights, out_width)
    out = out.reshape(reps, groups, CELLS)
    return out.transpose(1, 0, 2).reshape(groups, reps * CELLS)


def exact_dot(left, right):
    return jnp.dot(left, right, precision=lax.Precision.HIGHEST, preferred_element_type=jnp.float32)


def rake_own(county_tables, groups_in, age_rate, kind_rate):
    counties, width = county_tables.shape
    reps = width // CELLS
    span = counties * reps
    current = county_tables.reshape(counties, reps, CELLS).transpose(2, 0, 1)
    current = current.reshape(AGES, KINDS, span)
    age_goal = (age_rate * groups_in[:, None]).T
    age_goal = jnp.broadcast_to(age_goal[:, :, None], (AGES, counties, reps)).reshape(AGES, span)
    kind_goal = (kind_rate * groups_in[:, None]).T
    kind_goal = jnp.broadcast_to(kind_goal[:, :, None], (KINDS, counties, reps)).reshape(KINDS, span)
    age_factor = jnp.ones((AGES, span), jnp.float32)
    kind_factor = jnp.ones((KINDS, span), jnp.float32)
    for sweep_index in range(ITERS):
        ratios = age_goal / jnp.maximum(jnp.sum(current, axis=1), 1.0)
        current = current * ratios[:, None, :]
        age_factor = age_factor * ratios
        ratios = kind_goal / jnp.maximum(jnp.sum(current, axis=0), 1.0)
        current = current * ratios[None, :, :]
        kind_factor = kind_factor * ratios
    age_factor = age_factor.reshape(AGES, counties, reps).transpose(1, 2, 0).reshape(counties, reps * AGES)
    kind_factor = kind_factor.reshape(KINDS, counties, reps).transpose(1, 2, 0).reshape(counties, reps * KINDS)
    return jnp.concatenate([age_factor, kind_factor], axis=1)


def spreaders(reps):
    col = jnp.arange(reps * CELLS, dtype=jnp.int32)
    rep_of, cell_of = col // CELLS, col % CELLS
    age_row = jnp.arange(reps * AGES, dtype=jnp.int32)
    kind_row = jnp.arange(reps * KINDS, dtype=jnp.int32)
    to_age = ((age_row[:, None] // AGES == rep_of[None, :])
              & (age_row[:, None] % AGES == cell_of[None, :] // KINDS)).astype(jnp.float32)
    to_kind = ((kind_row[:, None] // KINDS == rep_of[None, :])
               & (kind_row[:, None] % KINDS == cell_of[None, :] % KINDS)).astype(jnp.float32)
    cell_sum = (cell_of[:, None] == jnp.arange(CELLS, dtype=jnp.int32)[None, :]).astype(jnp.float32)
    return to_age, to_kind, cell_sum


def local(weights, cell_ids, group_sizes, group_county, age_rate, kind_rate):
    tables = tabulate(weights, cell_ids, group_sizes)
    groups, width = tables.shape
    reps = width // CELLS
    county = group_county[:, 0]
    owners = lax.axis_size("rows")
    county_here = age_rate.shape[0]
    counties = county_here * owners
    county_range = jnp.arange(counties, dtype=jnp.int32)
    hits = county[None, :] == county_range[:, None]
    partial = exact_dot(hits.astype(jnp.float32), tables)
    present = jnp.sum(hits.astype(jnp.float32), axis=1).reshape(owners, 1, county_here)
    present = jnp.pad(present, ((0, 0), (0, 0), (0, width - county_here)))
    outgoing = jnp.concatenate([partial.reshape(owners, county_here, width), present], axis=1)
    half = width // 2
    core = lax.axis_index("rows") % 2
    low, high = outgoing[:, :, :half], outgoing[:, :, half:]
    keep = jnp.where(core == 0, low, high)
    give = jnp.where(core == 0, high, low)
    keep = keep + lax.ppermute(give, "rows", [(i, i ^ 1) for i in range(owners)])
    arrived = lax.all_to_all(
        keep.reshape(owners * (county_here + 1), half), "rows", 0, 0, tiled=True
    ).reshape(owners // 2, 2, county_here + 1, half)
    summed = jnp.sum(arrived, axis=0)
    county_tables = jnp.concatenate([summed[0, :county_here], summed[1, :county_here]], axis=1)
    groups_in = summed[0, county_here, :county_here]
    factors = rake_own(county_tables, groups_in, age_rate, kind_rate)
    sent = jnp.broadcast_to(factors[None], (owners,) + factors.shape)
    factors = lax.all_to_all(
        sent.reshape(owners * county_here, factors.shape[1]), "rows", 0, 0, tiled=True
    )
    mine = exact_dot(hits.T.astype(jnp.float32), factors)
    to_age, to_kind, cell_sum = spreaders(reps)
    factor = exact_dot(mine[:, :reps * AGES], to_age) * exact_dot(mine[:, reps * AGES:], to_kind)
    raked = tables * factor

    part_sum = exact_dot(raked, cell_sum)
    part_mean = part_sum / reps
    gap = raked - exact_dot(part_mean, cell_sum.T)
    part_m2 = exact_dot(jnp.square(gap), cell_sum)
    stats = jnp.concatenate([part_sum, part_m2], axis=1)
    shards = lax.axis_size("rep")
    sent = jnp.broadcast_to(stats[None], (shards,) + stats.shape)
    received = lax.all_to_all(
        sent.reshape(shards * groups, stats.shape[1]), "rep", 0, 0, tiled=True
    ).reshape(shards, groups, stats.shape[1])
    by_source = [received[source] for source in range(shards)]
    total_reps = reps * shards
    total = by_source[0][:, :CELLS]
    for source in range(1, shards):
        total = total + by_source[source][:, :CELLS]
    centre = total / total_reps
    deviation = None
    for source in range(shards):
        spread_in = by_source[source][:, CELLS:]
        off_centre = by_source[source][:, :CELLS] / reps - centre
        term = spread_in + reps * jnp.square(off_centre)
        deviation = term if deviation is None else deviation + term
    return (raked, deviation * (4.0 / total_reps))


def solution(mesh):
    placed = (
        P("rep", "rows"),
        P("rows"),
        P("rows", None),
        P("rows", None),
        P("rows", None),
        P("rows", None),
    )
    return jax.shard_map(
        local,
        mesh=mesh,
        in_specs=placed,
        out_specs=(P("rows", "rep"), P("rows", None)),
        check_vma=False,
    )
```

```python
import jax
import jax.numpy as jnp
from jax import lax
from jax.experimental import pallas as pl
from jax.experimental.pallas import tpu as pltpu
from jax.sharding import PartitionSpec as P

AGES = 4
KINDS = 8
CELLS = 32
LOW = 32
ITERS = 4
BLOCK = 256
SPAN = 12
USE_KERNEL = True


def tab_kernel(offs_ref, seg_ref, w_ref, out_ref):
    steps = seg_ref.shape[0]
    width = SPAN * CELLS
    out_ref[...] = jnp.zeros_like(out_ref)
    rows = lax.broadcasted_iota(jnp.int32, (width, BLOCK), 0)

    def body(b, carry):
        seg = seg_ref[pl.ds(b, 1), :]
        hot = (rows == seg).astype(jnp.bfloat16)
        start = pl.multiple_of(b * BLOCK, BLOCK)
        w = w_ref[:, pl.ds(start, BLOCK)]
        part = lax.dot_general(
            w, hot, (((1,), (1,)), ((), ())), preferred_element_type=jnp.float32
        )
        off = pl.multiple_of(offs_ref[b], 128)
        out_ref[:, pl.ds(off, width)] += part
        return carry

    lax.fori_loop(0, steps, body, 0, unroll=64)


def tab_plain(offs, seg, weights, out_width):
    reps = weights.shape[0]
    steps = seg.shape[0]
    width = SPAN * CELLS
    hot = (seg[:, None, :] == jnp.arange(width, dtype=jnp.int32)[None, :, None])
    w = weights.reshape(reps, steps, BLOCK)
    part = jnp.einsum("rbi,bni->brn", w.astype(jnp.float32), hot.astype(jnp.float32),
                      precision=lax.Precision.HIGHEST)
    cols = offs[:, None] + jnp.arange(width, dtype=jnp.int32)[None, :]
    out = jnp.zeros((reps, out_width), jnp.float32)
    return out.at[:, cols.reshape(-1)].add(part.transpose(1, 0, 2).reshape(reps, -1))


def tabulate(weights, cell_ids, group_sizes):
    reps, records = weights.shape
    sizes = group_sizes[0]
    groups = sizes.shape[0]
    ends = jnp.cumsum(sizes).astype(jnp.int32)
    steps = records // BLOCK
    block_start = jnp.arange(steps, dtype=jnp.int32) * BLOCK
    first = jnp.sum((ends[None, :] <= block_start[:, None]).astype(jnp.int32), axis=1)
    base = jnp.minimum(first - first % 4, groups - SPAN).astype(jnp.int32)
    group_range = jnp.arange(groups, dtype=jnp.int32)
    place = block_start[:, None] + jnp.arange(BLOCK, dtype=jnp.int32)[None, :]
    local = jnp.zeros((steps, BLOCK), jnp.int32)
    for j in range(SPAN - 1):
        chosen = group_range[None, :] == (base + j)[:, None]
        edge = jnp.sum(jnp.where(chosen, ends[None, :], 0), axis=1)
        edge = jnp.where(base + j < groups, edge, records + 1)
        local = local + (place >= edge[:, None]).astype(jnp.int32)
    seg = local * CELLS + cell_ids.reshape(steps, BLOCK)
    offs = (base * CELLS).astype(jnp.int32)
    out_width = groups * CELLS
    if USE_KERNEL:
        out = pl.pallas_call(
            tab_kernel,
            out_shape=jax.ShapeDtypeStruct((reps, out_width), jnp.float32),
            in_specs=[
                pl.BlockSpec(memory_space=pltpu.SMEM),
                pl.BlockSpec(memory_space=pltpu.VMEM),
                pl.BlockSpec(memory_space=pltpu.VMEM),
            ],
            out_specs=pl.BlockSpec(memory_space=pltpu.VMEM),
            cost_estimate=pl.CostEstimate(
                flops=2 * reps * records * SPAN * CELLS,
                bytes_accessed=weights.size * 2 + seg.size * 4 + reps * out_width * 4,
                transcendentals=0,
            ),
        )(offs, seg, weights)
    else:
        out = tab_plain(offs, seg, weights, out_width)
    out = out.reshape(reps, groups, CELLS)
    return out.transpose(1, 0, 2).reshape(groups, reps * CELLS)


def exact_dot(left, right):
    return jnp.dot(left, right, precision=lax.Precision.HIGHEST, preferred_element_type=jnp.float32)


def rake_own(county_tables, groups_in, age_rate, kind_rate):
    counties, width = county_tables.shape
    reps = width // CELLS
    span = counties * reps
    current = county_tables.reshape(counties, reps, CELLS).transpose(2, 0, 1)
    current = current.reshape(AGES, KINDS, span)
    age_goal = (age_rate * groups_in[:, None]).T
    age_goal = jnp.broadcast_to(age_goal[:, :, None], (AGES, counties, reps)).reshape(AGES, span)
    kind_goal = (kind_rate * groups_in[:, None]).T
    kind_goal = jnp.broadcast_to(kind_goal[:, :, None], (KINDS, counties, reps)).reshape(KINDS, span)
    age_factor = jnp.ones((AGES, span), jnp.float32)
    kind_factor = jnp.ones((KINDS, span), jnp.float32)
    for sweep_index in range(ITERS):
        ratios = age_goal / jnp.maximum(jnp.sum(current, axis=1), 1.0)
        current = current * ratios[:, None, :]
        age_factor = age_factor * ratios
        ratios = kind_goal / jnp.maximum(jnp.sum(current, axis=0), 1.0)
        current = current * ratios[None, :, :]
        kind_factor = kind_factor * ratios
    age_factor = age_factor.reshape(AGES, counties, reps).transpose(1, 2, 0).reshape(counties, reps * AGES)
    kind_factor = kind_factor.reshape(KINDS, counties, reps).transpose(1, 2, 0).reshape(counties, reps * KINDS)
    return jnp.concatenate([age_factor, kind_factor], axis=1)


def spreaders(reps):
    col = jnp.arange(reps * CELLS, dtype=jnp.int32)
    rep_of, cell_of = col // CELLS, col % CELLS
    age_row = jnp.arange(reps * AGES, dtype=jnp.int32)
    kind_row = jnp.arange(reps * KINDS, dtype=jnp.int32)
    to_age = ((age_row[:, None] // AGES == rep_of[None, :])
              & (age_row[:, None] % AGES == cell_of[None, :] // KINDS)).astype(jnp.float32)
    to_kind = ((kind_row[:, None] // KINDS == rep_of[None, :])
               & (kind_row[:, None] % KINDS == cell_of[None, :] % KINDS)).astype(jnp.float32)
    cell_sum = (cell_of[:, None] == jnp.arange(CELLS, dtype=jnp.int32)[None, :]).astype(jnp.float32)
    return to_age, to_kind, cell_sum


def local(weights, cell_ids, group_sizes, group_county, age_rate, kind_rate):
    tables = tabulate(weights, cell_ids, group_sizes)
    groups, width = tables.shape
    reps = width // CELLS
    county = group_county[:, 0]
    owners = lax.axis_size("rows")
    county_here = age_rate.shape[0]
    counties = county_here * owners
    county_range = jnp.arange(counties, dtype=jnp.int32)
    hits = county[None, :] == county_range[:, None]
    partial = exact_dot(hits.astype(jnp.float32), tables)
    present = jnp.sum(hits.astype(jnp.float32), axis=1).reshape(owners, 1, county_here)
    present = jnp.pad(present, ((0, 0), (0, 0), (0, width - county_here)))
    outgoing = jnp.concatenate([partial.reshape(owners, county_here, width), present], axis=1)
    half = width // 2
    core = lax.axis_index("rows") % 2
    low, high = outgoing[:, :, :half], outgoing[:, :, half:]
    keep = jnp.where(core == 0, low, high)
    give = jnp.where(core == 0, high, low)
    keep = keep + lax.ppermute(give, "rows", [(i, i ^ 1) for i in range(owners)])
    arrived = lax.all_to_all(
        keep.reshape(owners * (county_here + 1), half), "rows", 0, 0, tiled=True
    ).reshape(owners // 2, 2, county_here + 1, half)
    summed = jnp.sum(arrived, axis=0)
    county_tables = jnp.concatenate([summed[0, :county_here], summed[1, :county_here]], axis=1)
    groups_in = summed[0, county_here, :county_here]
    factors = rake_own(county_tables, groups_in, age_rate, kind_rate)
    sent = jnp.broadcast_to(factors[None], (owners,) + factors.shape)
    factors = lax.all_to_all(
        sent.reshape(owners * county_here, factors.shape[1]), "rows", 0, 0, tiled=True
    )
    mine = exact_dot(hits.T.astype(jnp.float32), factors)
    to_age, to_kind, cell_sum = spreaders(reps)
    factor = exact_dot(mine[:, :reps * AGES], to_age) * exact_dot(mine[:, reps * AGES:], to_kind)
    raked = tables * factor

    part_sum = exact_dot(raked, cell_sum)
    part_mean = part_sum / reps
    gap = raked - exact_dot(part_mean, cell_sum.T)
    part_m2 = exact_dot(jnp.square(gap), cell_sum)
    stats = jnp.concatenate([part_sum, part_m2], axis=1)
    shards = lax.axis_size("rep")
    me = lax.axis_index("rep")
    received = [stats] + [
        lax.ppermute(stats, "rep", [(i, (i + s) % shards) for i in range(shards)])
        for s in range(1, shards)
    ]
    by_source = []
    for source in range(shards):
        value = jnp.zeros_like(stats)
        for s in range(shards):
            value = jnp.where((me - s) % shards == source, received[s], value)
        by_source.append(value)
    total_reps = reps * shards
    total = by_source[0][:, :CELLS]
    for source in range(1, shards):
        total = total + by_source[source][:, :CELLS]
    centre = total / total_reps
    deviation = None
    for source in range(shards):
        spread_in = by_source[source][:, CELLS:]
        off_centre = by_source[source][:, :CELLS] / reps - centre
        term = spread_in + reps * jnp.square(off_centre)
        deviation = term if deviation is None else deviation + term
    return (raked, deviation * (4.0 / total_reps))


def solution(mesh):
    placed = (
        P("rep", "rows"),
        P("rows"),
        P("rows", None),
        P("rows", None),
        P("rows", None),
        P("rows", None),
    )
    return jax.shard_map(
        local,
        mesh=mesh,
        in_specs=placed,
        out_specs=(P("rows", "rep"), P("rows", None)),
        check_vma=False,
    )
```

```python
import jax
import jax.numpy as jnp
from jax import lax
from jax.experimental import pallas as pl
from jax.experimental.pallas import tpu as pltpu
from jax.sharding import PartitionSpec as P

AGES = 4
KINDS = 8
CELLS = 32
LOW = 32
ITERS = 4
BLOCK = 512
SPAN = 20
USE_KERNEL = True


def tab_kernel(offs_ref, seg_ref, w_ref, out_ref):
    steps = seg_ref.shape[0]
    width = SPAN * CELLS
    out_ref[...] = jnp.zeros_like(out_ref)
    rows = lax.broadcasted_iota(jnp.int32, (width, BLOCK), 0)

    def body(b, carry):
        seg = seg_ref[pl.ds(b, 1), :]
        hot = (rows == seg).astype(jnp.bfloat16)
        start = pl.multiple_of(b * BLOCK, BLOCK)
        w = w_ref[:, pl.ds(start, BLOCK)]
        part = lax.dot_general(
            w, hot, (((1,), (1,)), ((), ())), preferred_element_type=jnp.float32
        )
        off = pl.multiple_of(offs_ref[b], 128)
        out_ref[:, pl.ds(off, width)] += part
        return carry

    lax.fori_loop(0, steps, body, 0, unroll=32)


def tab_plain(offs, seg, weights, out_width):
    reps = weights.shape[0]
    steps = seg.shape[0]
    width = SPAN * CELLS
    hot = (seg[:, None, :] == jnp.arange(width, dtype=jnp.int32)[None, :, None])
    w = weights.reshape(reps, steps, BLOCK)
    part = jnp.einsum("rbi,bni->brn", w.astype(jnp.float32), hot.astype(jnp.float32),
                      precision=lax.Precision.HIGHEST)
    cols = offs[:, None] + jnp.arange(width, dtype=jnp.int32)[None, :]
    out = jnp.zeros((reps, out_width), jnp.float32)
    return out.at[:, cols.reshape(-1)].add(part.transpose(1, 0, 2).reshape(reps, -1))


def tabulate(weights, cell_ids, group_sizes):
    reps, records = weights.shape
    sizes = group_sizes[0]
    groups = sizes.shape[0]
    ends = jnp.cumsum(sizes).astype(jnp.int32)
    steps = records // BLOCK
    block_start = jnp.arange(steps, dtype=jnp.int32) * BLOCK
    first = jnp.sum((ends[None, :] <= block_start[:, None]).astype(jnp.int32), axis=1)
    base = jnp.minimum(first - first % 4, groups - SPAN).astype(jnp.int32)
    group_range = jnp.arange(groups, dtype=jnp.int32)
    place = block_start[:, None] + jnp.arange(BLOCK, dtype=jnp.int32)[None, :]
    local = jnp.zeros((steps, BLOCK), jnp.int32)
    for j in range(SPAN - 1):
        chosen = group_range[None, :] == (base + j)[:, None]
        edge = jnp.sum(jnp.where(chosen, ends[None, :], 0), axis=1)
        edge = jnp.where(base + j < groups, edge, records + 1)
        local = local + (place >= edge[:, None]).astype(jnp.int32)
    seg = local * CELLS + cell_ids.reshape(steps, BLOCK)
    offs = (base * CELLS).astype(jnp.int32)
    out_width = groups * CELLS
    if USE_KERNEL:
        out = pl.pallas_call(
            tab_kernel,
            out_shape=jax.ShapeDtypeStruct((reps, out_width), jnp.float32),
            in_specs=[
                pl.BlockSpec(memory_space=pltpu.SMEM),
                pl.BlockSpec(memory_space=pltpu.VMEM),
                pl.BlockSpec(memory_space=pltpu.VMEM),
            ],
            out_specs=pl.BlockSpec(memory_space=pltpu.VMEM),
            cost_estimate=pl.CostEstimate(
                flops=2 * reps * records * SPAN * CELLS,
                bytes_accessed=weights.size * 2 + seg.size * 4 + reps * out_width * 4,
                transcendentals=0,
            ),
        )(offs, seg, weights)
    else:
        out = tab_plain(offs, seg, weights, out_width)
    out = out.reshape(reps, groups, CELLS)
    return out.transpose(1, 0, 2).reshape(groups, reps * CELLS)


def exact_dot(left, right):
    return jnp.dot(left, right, precision=lax.Precision.HIGHEST, preferred_element_type=jnp.float32)


def rake_own(county_tables, groups_in, age_rate, kind_rate):
    counties, width = county_tables.shape
    reps = width // CELLS
    span = counties * reps
    current = county_tables.reshape(counties, reps, CELLS).transpose(2, 0, 1)
    current = current.reshape(AGES, KINDS, span)
    age_goal = (age_rate * groups_in[:, None]).T
    age_goal = jnp.broadcast_to(age_goal[:, :, None], (AGES, counties, reps)).reshape(AGES, span)
    kind_goal = (kind_rate * groups_in[:, None]).T
    kind_goal = jnp.broadcast_to(kind_goal[:, :, None], (KINDS, counties, reps)).reshape(KINDS, span)
    age_factor = jnp.ones((AGES, span), jnp.float32)
    kind_factor = jnp.ones((KINDS, span), jnp.float32)
    for sweep_index in range(ITERS):
        ratios = age_goal / jnp.maximum(jnp.sum(current, axis=1), 1.0)
        current = current * ratios[:, None, :]
        age_factor = age_factor * ratios
        ratios = kind_goal / jnp.maximum(jnp.sum(current, axis=0), 1.0)
        current = current * ratios[None, :, :]
        kind_factor = kind_factor * ratios
    age_factor = age_factor.reshape(AGES, counties, reps).transpose(1, 2, 0).reshape(counties, reps * AGES)
    kind_factor = kind_factor.reshape(KINDS, counties, reps).transpose(1, 2, 0).reshape(counties, reps * KINDS)
    return jnp.concatenate([age_factor, kind_factor], axis=1)


def spreaders(reps):
    col = jnp.arange(reps * CELLS, dtype=jnp.int32)
    rep_of, cell_of = col // CELLS, col % CELLS
    age_row = jnp.arange(reps * AGES, dtype=jnp.int32)
    kind_row = jnp.arange(reps * KINDS, dtype=jnp.int32)
    to_age = ((age_row[:, None] // AGES == rep_of[None, :])
              & (age_row[:, None] % AGES == cell_of[None, :] // KINDS)).astype(jnp.float32)
    to_kind = ((kind_row[:, None] // KINDS == rep_of[None, :])
               & (kind_row[:, None] % KINDS == cell_of[None, :] % KINDS)).astype(jnp.float32)
    cell_sum = (cell_of[:, None] == jnp.arange(CELLS, dtype=jnp.int32)[None, :]).astype(jnp.float32)
    return to_age, to_kind, cell_sum


def local(weights, cell_ids, group_sizes, group_county, age_rate, kind_rate):
    tables = tabulate(weights, cell_ids, group_sizes)
    groups, width = tables.shape
    reps = width // CELLS
    county = group_county[:, 0]
    owners = lax.axis_size("rows")
    county_here = age_rate.shape[0]
    counties = county_here * owners
    county_range = jnp.arange(counties, dtype=jnp.int32)
    hits = county[None, :] == county_range[:, None]
    partial = exact_dot(hits.astype(jnp.float32), tables)
    present = jnp.sum(hits.astype(jnp.float32), axis=1).reshape(owners, 1, county_here)
    present = jnp.pad(present, ((0, 0), (0, 0), (0, width - county_here)))
    outgoing = jnp.concatenate([partial.reshape(owners, county_here, width), present], axis=1)
    half = width // 2
    core = lax.axis_index("rows") % 2
    low, high = outgoing[:, :, :half], outgoing[:, :, half:]
    keep = jnp.where(core == 0, low, high)
    give = jnp.where(core == 0, high, low)
    keep = keep + lax.ppermute(give, "rows", [(i, i ^ 1) for i in range(owners)])
    arrived = lax.all_to_all(
        keep.reshape(owners * (county_here + 1), half), "rows", 0, 0, tiled=True
    ).reshape(owners // 2, 2, county_here + 1, half)
    summed = jnp.sum(arrived, axis=0)
    county_tables = jnp.concatenate([summed[0, :county_here], summed[1, :county_here]], axis=1)
    groups_in = summed[0, county_here, :county_here]
    factors = rake_own(county_tables, groups_in, age_rate, kind_rate)
    sent = jnp.broadcast_to(factors[None], (owners,) + factors.shape)
    factors = lax.all_to_all(
        sent.reshape(owners * county_here, factors.shape[1]), "rows", 0, 0, tiled=True
    )
    mine = exact_dot(hits.T.astype(jnp.float32), factors)
    to_age, to_kind, cell_sum = spreaders(reps)
    factor = exact_dot(mine[:, :reps * AGES], to_age) * exact_dot(mine[:, reps * AGES:], to_kind)
    raked = tables * factor

    part_sum = exact_dot(raked, cell_sum)
    part_mean = part_sum / reps
    gap = raked - exact_dot(part_mean, cell_sum.T)
    part_m2 = exact_dot(jnp.square(gap), cell_sum)
    stats = jnp.concatenate([part_sum, part_m2], axis=1)
    shards = lax.axis_size("rep")
    me = lax.axis_index("rep")
    received = [stats] + [
        lax.ppermute(stats, "rep", [(i, (i + s) % shards) for i in range(shards)])
        for s in range(1, shards)
    ]
    by_source = []
    for source in range(shards):
        value = jnp.zeros_like(stats)
        for s in range(shards):
            value = jnp.where((me - s) % shards == source, received[s], value)
        by_source.append(value)
    total_reps = reps * shards
    total = by_source[0][:, :CELLS]
    for source in range(1, shards):
        total = total + by_source[source][:, :CELLS]
    centre = total / total_reps
    deviation = None
    for source in range(shards):
        spread_in = by_source[source][:, CELLS:]
        off_centre = by_source[source][:, :CELLS] / reps - centre
        term = spread_in + reps * jnp.square(off_centre)
        deviation = term if deviation is None else deviation + term
    return (raked, deviation * (4.0 / total_reps))


def solution(mesh):
    placed = (
        P("rep", "rows"),
        P("rows"),
        P("rows", None),
        P("rows", None),
        P("rows", None),
        P("rows", None),
    )
    return jax.shard_map(
        local,
        mesh=mesh,
        in_specs=placed,
        out_specs=(P("rows", "rep"), P("rows", None)),
        check_vma=False,
    )
```

```python
import jax
import jax.numpy as jnp
from jax import lax
from jax.experimental import pallas as pl
from jax.experimental.pallas import tpu as pltpu
from jax.sharding import PartitionSpec as P

AGES = 4
KINDS = 8
CELLS = 32
LOW = 32
ITERS = 4
BLOCK = 256
SPAN = 12
USE_KERNEL = True


def tab_kernel(offs_ref, seg_ref, w_ref, out_ref):
    steps = seg_ref.shape[0]
    width = SPAN * CELLS
    out_ref[...] = jnp.zeros_like(out_ref)
    rows = lax.broadcasted_iota(jnp.int32, (width, BLOCK), 0)

    def body(b, carry):
        seg = seg_ref[pl.ds(b, 1), :]
        hot = (rows == seg).astype(jnp.bfloat16)
        start = pl.multiple_of(b * BLOCK, BLOCK)
        w = w_ref[:, pl.ds(start, BLOCK)]
        part = lax.dot_general(
            w, hot, (((1,), (1,)), ((), ())), preferred_element_type=jnp.float32
        )
        off = pl.multiple_of(offs_ref[b], 128)
        out_ref[:, pl.ds(off, width)] += part
        return carry

    lax.fori_loop(0, steps, body, 0, unroll=64)


def tab_plain(offs, seg, weights, out_width):
    reps = weights.shape[0]
    steps = seg.shape[0]
    width = SPAN * CELLS
    hot = (seg[:, None, :] == jnp.arange(width, dtype=jnp.int32)[None, :, None])
    w = weights.reshape(reps, steps, BLOCK)
    part = jnp.einsum("rbi,bni->brn", w.astype(jnp.float32), hot.astype(jnp.float32),
                      precision=lax.Precision.HIGHEST)
    cols = offs[:, None] + jnp.arange(width, dtype=jnp.int32)[None, :]
    out = jnp.zeros((reps, out_width), jnp.float32)
    return out.at[:, cols.reshape(-1)].add(part.transpose(1, 0, 2).reshape(reps, -1))


def tabulate(weights, cell_ids, group_sizes):
    reps, records = weights.shape
    sizes = group_sizes[0]
    groups = sizes.shape[0]
    ends = jnp.cumsum(sizes).astype(jnp.int32)
    steps = records // BLOCK
    block_start = jnp.arange(steps, dtype=jnp.int32) * BLOCK
    first = jnp.sum((ends[None, :] <= block_start[:, None]).astype(jnp.int32), axis=1)
    base = jnp.minimum(first - first % 4, groups - SPAN).astype(jnp.int32)
    group_range = jnp.arange(groups, dtype=jnp.int32)
    place = block_start[:, None] + jnp.arange(BLOCK, dtype=jnp.int32)[None, :]
    local = jnp.zeros((steps, BLOCK), jnp.int32)
    for j in range(SPAN - 1):
        chosen = group_range[None, :] == (base + j)[:, None]
        edge = jnp.sum(jnp.where(chosen, ends[None, :], 0), axis=1)
        edge = jnp.where(base + j < groups, edge, records + 1)
        local = local + (place >= edge[:, None]).astype(jnp.int32)
    seg = local * CELLS + cell_ids.reshape(steps, BLOCK)
    offs = (base * CELLS).astype(jnp.int32)
    out_width = groups * CELLS
    if USE_KERNEL:
        out = pl.pallas_call(
            tab_kernel,
            out_shape=jax.ShapeDtypeStruct((reps, out_width), jnp.float32),
            in_specs=[
                pl.BlockSpec(memory_space=pltpu.SMEM),
                pl.BlockSpec(memory_space=pltpu.VMEM),
                pl.BlockSpec(memory_space=pltpu.VMEM),
            ],
            out_specs=pl.BlockSpec(memory_space=pltpu.VMEM),
            cost_estimate=pl.CostEstimate(
                flops=2 * reps * records * SPAN * CELLS,
                bytes_accessed=weights.size * 2 + seg.size * 4 + reps * out_width * 4,
                transcendentals=0,
            ),
        )(offs, seg, weights)
    else:
        out = tab_plain(offs, seg, weights, out_width)
    out = out.reshape(reps, groups, CELLS)
    return out.transpose(1, 0, 2).reshape(groups, reps * CELLS)


def exact_dot(left, right):
    return jnp.dot(left, right, precision=lax.Precision.HIGHEST, preferred_element_type=jnp.float32)


def rake_own(county_tables, groups_in, age_rate, kind_rate):
    counties, width = county_tables.shape
    reps = width // CELLS
    span = counties * reps
    current = county_tables.reshape(counties, reps, CELLS).transpose(2, 0, 1)
    current = current.reshape(AGES, KINDS, span)
    age_goal = (age_rate * groups_in[:, None]).T
    age_goal = jnp.broadcast_to(age_goal[:, :, None], (AGES, counties, reps)).reshape(AGES, span)
    kind_goal = (kind_rate * groups_in[:, None]).T
    kind_goal = jnp.broadcast_to(kind_goal[:, :, None], (KINDS, counties, reps)).reshape(KINDS, span)
    age_factor = jnp.ones((AGES, span), jnp.float32)
    kind_factor = jnp.ones((KINDS, span), jnp.float32)
    for sweep_index in range(ITERS):
        ratios = age_goal / jnp.maximum(jnp.sum(current, axis=1), 1.0)
        current = current * ratios[:, None, :]
        age_factor = age_factor * ratios
        ratios = kind_goal / jnp.maximum(jnp.sum(current, axis=0), 1.0)
        current = current * ratios[None, :, :]
        kind_factor = kind_factor * ratios
    age_factor = age_factor.reshape(AGES, counties, reps).transpose(1, 2, 0).reshape(counties, reps * AGES)
    kind_factor = kind_factor.reshape(KINDS, counties, reps).transpose(1, 2, 0).reshape(counties, reps * KINDS)
    return jnp.concatenate([age_factor, kind_factor], axis=1)


def spreaders(reps):
    col = jnp.arange(reps * CELLS, dtype=jnp.int32)
    rep_of, cell_of = col // CELLS, col % CELLS
    age_row = jnp.arange(reps * AGES, dtype=jnp.int32)
    kind_row = jnp.arange(reps * KINDS, dtype=jnp.int32)
    to_age = ((age_row[:, None] // AGES == rep_of[None, :])
              & (age_row[:, None] % AGES == cell_of[None, :] // KINDS)).astype(jnp.float32)
    to_kind = ((kind_row[:, None] // KINDS == rep_of[None, :])
               & (kind_row[:, None] % KINDS == cell_of[None, :] % KINDS)).astype(jnp.float32)
    cell_sum = (cell_of[:, None] == jnp.arange(CELLS, dtype=jnp.int32)[None, :]).astype(jnp.float32)
    return to_age, to_kind, cell_sum


def local(weights, cell_ids, group_sizes, group_county, age_rate, kind_rate):
    tables = tabulate(weights, cell_ids, group_sizes)
    groups, width = tables.shape
    reps = width // CELLS
    county = group_county[:, 0]
    owners = lax.axis_size("rows")
    county_here = age_rate.shape[0]
    counties = county_here * owners
    county_range = jnp.arange(counties, dtype=jnp.int32)
    hits = county[None, :] == county_range[:, None]
    partial = exact_dot(hits.astype(jnp.float32), tables)
    present = jnp.sum(hits.astype(jnp.float32), axis=1).reshape(owners, 1, county_here)
    present = jnp.pad(present, ((0, 0), (0, 0), (0, width - county_here)))
    outgoing = jnp.concatenate([partial.reshape(owners, county_here, width), present], axis=1)
    half = width // 2
    core = lax.axis_index("rows") % 2
    low, high = outgoing[:, :, :half], outgoing[:, :, half:]
    keep = jnp.where(core == 0, low, high)
    give = jnp.where(core == 0, high, low)
    keep = keep + lax.ppermute(give, "rows", [(i, i ^ 1) for i in range(owners)])
    arrived = lax.all_to_all(
        keep.reshape(owners * (county_here + 1), half), "rows", 0, 0, tiled=True
    ).reshape(owners // 2, 2, county_here + 1, half)
    summed = jnp.sum(arrived, axis=0)
    county_tables = jnp.concatenate([summed[0, :county_here], summed[1, :county_here]], axis=1)
    groups_in = summed[0, county_here, :county_here]
    factors = rake_own(county_tables, groups_in, age_rate, kind_rate)
    factors = jnp.pad(factors, ((0, 0), (0, (-factors.shape[1]) % 128)))
    sent = jnp.broadcast_to(factors[None], (owners,) + factors.shape)
    factors = lax.all_to_all(
        sent.reshape(owners * county_here, factors.shape[1]), "rows", 0, 0, tiled=True
    )
    mine = exact_dot(hits.T.astype(jnp.float32), factors)
    to_age, to_kind, cell_sum = spreaders(reps)
    factor = exact_dot(mine[:, :reps * AGES], to_age) * exact_dot(mine[:, reps * AGES:reps * (AGES + KINDS)], to_kind)
    raked = tables * factor

    part_sum = exact_dot(raked, cell_sum)
    part_mean = part_sum / reps
    gap = raked - exact_dot(part_mean, cell_sum.T)
    part_m2 = exact_dot(jnp.square(gap), cell_sum)
    stats = jnp.concatenate([part_sum, part_m2], axis=1)
    shards = lax.axis_size("rep")
    me = lax.axis_index("rep")
    received = [stats] + [
        lax.ppermute(stats, "rep", [(i, (i + s) % shards) for i in range(shards)])
        for s in range(1, shards)
    ]
    by_source = []
    for source in range(shards):
        value = jnp.zeros_like(stats)
        for s in range(shards):
            value = jnp.where((me - s) % shards == source, received[s], value)
        by_source.append(value)
    total_reps = reps * shards
    total = by_source[0][:, :CELLS]
    for source in range(1, shards):
        total = total + by_source[source][:, :CELLS]
    centre = total / total_reps
    deviation = None
    for source in range(shards):
        spread_in = by_source[source][:, CELLS:]
        off_centre = by_source[source][:, :CELLS] / reps - centre
        term = spread_in + reps * jnp.square(off_centre)
        deviation = term if deviation is None else deviation + term
    return (raked, deviation * (4.0 / total_reps))


def solution(mesh):
    placed = (
        P("rep", "rows"),
        P("rows"),
        P("rows", None),
        P("rows", None),
        P("rows", None),
        P("rows", None),
    )
    return jax.shard_map(
        local,
        mesh=mesh,
        in_specs=placed,
        out_specs=(P("rows", "rep"), P("rows", None)),
        check_vma=False,
    )
```
